512 devices in a mesh: comp: 32 (over z, core), feat: 16 (over x, y).
Axes of the slice: x: 4, y: 4, z: 16, core: 2. Of those that a mesh axis runs over, the one named last changes fastest.
Arguments:
- block_values: bfloat16 [32, 16, 24, 128, 128], P('comp', 'feat'), may hold values from -0.0625 to 0.0625
- block_rows: int32 [32, 16, 24], P('comp', 'feat'), may hold values from 0 to 15, as said below
- block_cols: int32 [32, 16, 24], P('comp', 'feat'), may hold values from 0 to 13, as said below
- block_counts: int32 [32, 16], P('comp', 'feat'), may hold values from 8 to 24, as said below
- right_side: float32 [65536, 128], P(('comp', 'feat')), may hold values from -6 to 6
- ridge: float32 [128], replicated, may hold values from 0.1 to 2
Outputs:
- solution: float32 [28672, 128], P('feat')
- residual: float32 [65536, 128], P(('comp', 'feat'))
The draws below stay inside these ranges and needn't reach their ends.
Inputs may be any that keep to these rules, and one draw needn't show every extreme that they name: Within one device the listed (block_rows, block_cols) pairs of all 24 slots are distinct; block rows are very uneven in how many blocks they hold. `block_cols`: see block_rows. `block_counts`: slots at or beyond a device's count are ignored; some device is full in every draw.
All inputs are finite; a program needn't handle non-finite values.
Results may differ from the reference program's by a relative error of at most 0.0029.
Values may be sent and summed in bfloat16 or wider, within the bound.
No kernel may reach another device: no remote copies, remote signals or barrier semaphores. Data moves between devices by JAX's collectives and lax.ppermute only.
A program may use at most 64 MiB of HBM per device.

```python
import math
import jax
import jax.numpy as jnp
from jax import lax

BLOCK = 128
RESP = 128
RB_DEV = 16
CB_DEV = 14
BLK_DEV = 24
ITERS = 2
COMPS = 65536
FEATS = 28672
N_COMP = 32
N_FEAT = 16


def coordinate_table(key):
    heavy_key = jax.random.fold_in(key, 11)
    noise_key = jax.random.fold_in(key, 12)
    positions = RB_DEV * CB_DEV
    heavy = jax.random.randint(heavy_key, (N_COMP, N_FEAT, RB_DEV), 0, 4)
    noise = jax.random.randint(noise_key, (N_COMP, N_FEAT, positions), 0, 1000)
    row_of = jnp.arange(positions) // CB_DEV
    score = (jnp.take(heavy, row_of, axis=2) * 1000 + noise) * positions + jnp.arange(positions)
    _, order = lax.top_k(score, BLK_DEV)
    return ((order // CB_DEV).astype(jnp.int32), (order % CB_DEV).astype(jnp.int32))


def draw_block_rows(key, part):
    return coordinate_table(key)[0]


def draw_block_cols(key, part):
    return coordinate_table(key)[1]


def draw_block_counts(key, part):
    base = jax.random.randint(jax.random.fold_in(key, 21), (N_COMP * N_FEAT,), max(1, BLK_DEV // 3), BLK_DEV + 1)
    chosen = jax.random.randint(jax.random.fold_in(key, 22), (), 0, N_COMP * N_FEAT)
    full = jnp.where(jnp.arange(N_COMP * N_FEAT) == chosen, BLK_DEV, base)
    return full.reshape(N_COMP, N_FEAT).astype(jnp.int32)


def steps_of(stream_key, shape, split, smallest, largest):
    factor_of, own = 1.0, jax.random.fold_in(stream_key, 6)
    for axis_at, shards_of in split:
        heights = jnp.exp(jax.random.uniform(jax.random.fold_in(own, axis_at), (shards_of,), jnp.float32, smallest / len(split), largest / len(split)))
        factor_of = factor_of * jnp.repeat(heights, shape[axis_at] // shards_of).reshape([-1 if axis == axis_at else 1 for axis in range(len(shape))])
    return factor_of


def scatter_about(rng, extent, width, reach, shards=(), kind=jnp.bfloat16):
    array = jax.random.normal(rng, extent, jnp.float32) * width
    if len(shards) > 0:
        array = steps_of(rng, extent, shards, -0.22, 0.18) * array
    return jnp.clip(array, min=-reach, max=reach).astype(kind)


def setup_inputs(seed: int = 0) -> dict:
    keys = jax.random.split(jax.random.key(seed), 7)
    return {
        "block_values": scatter_about(keys[0], (N_COMP, N_FEAT, BLK_DEV, BLOCK, BLOCK), (BLOCK * BLK_DEV * N_COMP // CB_DEV) ** -0.5, 0.0625, ((0, 32), (1, 16))),
        "block_rows": draw_block_rows(jax.random.fold_in(keys[6], 71), 0),
        "block_cols": draw_block_cols(jax.random.fold_in(keys[6], 71), 0),
        "block_counts": draw_block_counts(jax.random.fold_in(keys[6], 71), 0),
        "right_side": scatter_about(keys[4], (COMPS, RESP), 1.0, 6.0, ((0, 512),), jnp.float32),
        "ridge": jnp.clip(jnp.exp(jax.random.uniform(keys[5], (RESP,), jnp.float32, math.log(0.1), math.log(2.0))), 0.1, 2.0),
    }


def rounded(matrix):
    return lax.optimization_barrier(matrix.astype(jnp.bfloat16))


def reference(block_values, block_rows, block_cols, block_counts, right_side, ridge):
    responses = right_side.shape[1]
    slot_live = (jnp.arange(BLK_DEV)[None, None, :] < block_counts[:, :, None]).astype(jnp.float32)
    feat_index = jnp.arange(N_FEAT)[:, None]

    def forward(low_panel):
        col_panels = low_panel.reshape(N_FEAT, CB_DEV, BLOCK, responses)

        def per_comp(comp_index):
            selected = col_panels[feat_index, block_cols[comp_index]].astype(jnp.float32)
            block_products = jnp.einsum("fsij,fsjk->fsik", block_values[comp_index].astype(jnp.float32), selected)
            row_lookup_table = (block_rows[comp_index][:, :, None] == jnp.arange(RB_DEV)[None, None, :]).astype(jnp.float32)
            row_lookup_table = row_lookup_table * slot_live[comp_index][:, :, None]
            return jnp.einsum("vmt,vmyj->tyj", row_lookup_table, block_products, precision=lax.Precision.HIGHEST)

        return lax.map(per_comp, jnp.arange(N_COMP)).reshape(COMPS, responses)

    def backward(low_slab):
        row_slabs = low_slab.reshape(N_COMP, RB_DEV, BLOCK, responses)

        def per_comp(running_accumulator, comp_index):
            selected = row_slabs[comp_index][block_rows[comp_index]].astype(jnp.float32)
            block_products = jnp.einsum("fsij,fsik->fsjk", block_values[comp_index].astype(jnp.float32), selected)
            col_table = (block_cols[comp_index][:, :, None] == jnp.arange(CB_DEV)[None, None, :]).astype(jnp.float32)
            col_table = col_table * slot_live[comp_index][:, :, None]
            added = jnp.einsum("fsq,fsjk->fqjk", col_table, block_products, precision=lax.Precision.HIGHEST)
            return running_accumulator + added, 0

        start = jnp.zeros((N_FEAT, CB_DEV, BLOCK, responses), jnp.float32)
        total, _ = lax.scan(per_comp, start, jnp.arange(N_COMP))
        return total.reshape(FEATS, responses)

    residual = right_side
    solution = jnp.zeros((FEATS, responses), jnp.float32)
    gradient = backward(rounded(residual))
    energy = jnp.sum(gradient * gradient, axis=0)
    search_direction = gradient
    for step_index in range(ITERS):
        image_rows = forward(rounded(search_direction))
        curvature = jnp.sum(image_rows * image_rows, axis=0) + ridge * jnp.sum(search_direction * search_direction, axis=0)
        step_size = energy / curvature
        solution = solution + step_size * search_direction
        residual = residual - step_size * image_rows
        if step_index + 1 < ITERS:
            gradient = backward(rounded(residual)) - ridge * solution
            next_energy = jnp.sum(gradient * gradient, axis=0)
            search_direction = gradient + (next_energy / energy) * search_direction
            energy = next_energy
    return solution, residual
```

```python
import jax
import jax.numpy as jnp
from jax import lax
from jax.sharding import PartitionSpec as P

RB_DEV = 16
CB_DEV = 14
ITERS = 2


def reduce_over(partial, axis, parts):
    rows = partial.shape[0] // parts
    pieces = partial.reshape(parts, rows, *partial.shape[1:])
    return lax.all_to_all(pieces, axis, 0, 0, tiled=True).sum(0)


def total_over_mesh(stacked, n_comp, n_feat):
    spread = jnp.broadcast_to(stacked[None], (n_feat,) + stacked.shape)
    by_feat = lax.all_to_all(spread, "feat", 0, 0, tiled=True).sum(0)
    spread = jnp.broadcast_to(by_feat[None], (n_comp,) + stacked.shape)
    return lax.all_to_all(spread, "comp", 0, 0, tiled=True).sum(0)


def shards(block_values, block_rows, block_cols, block_counts, right_side, ridge, n_comp, n_feat):
    values = block_values[0, 0]
    slot_rows = block_rows[0, 0]
    slot_cols = block_cols[0, 0]
    count_of_slots = block_counts[0, 0]
    responses = right_side.shape[1]
    total_slot_number = values.shape[0]
    block_edge = values.shape[1]
    feat_rows = CB_DEV * block_edge
    own_rows = feat_rows // n_comp
    comp_index = lax.axis_index("comp")
    slot_live = (jnp.arange(total_slot_number) < count_of_slots).astype(jnp.float32)
    row_lookup_table = (jnp.arange(RB_DEV)[:, None] == slot_rows[None, :]).astype(
        jnp.float32
    ) * slot_live[None, :]
    col_table = (jnp.arange(CB_DEV)[:, None] == slot_cols[None, :]).astype(jnp.float32) * slot_live[
        None, :
    ]

    def backward(low_slab):
        row_slabs = low_slab.reshape(RB_DEV, block_edge, responses)
        selected = jnp.take(row_slabs, slot_rows, axis=0)
        block_products = jnp.einsum(
            "sij,sik->sjk", values, selected, preferred_element_type=jnp.float32
        )
        summed = jnp.einsum(
            "qs,sjk->qjk", col_table, block_products, precision=lax.Precision.HIGHEST
        )
        return summed.reshape(feat_rows, responses)

    def forward(direction):
        col_panels = direction.astype(jnp.bfloat16).reshape(CB_DEV, block_edge, responses)
        forward_selected = jnp.take(col_panels, slot_cols, axis=0)
        forward_block_products = jnp.einsum(
            "sij,sjk->sik", values, forward_selected, preferred_element_type=jnp.float32
        )
        forward_summed = jnp.einsum(
            "rs,sik->rik", row_lookup_table, forward_block_products, precision=lax.Precision.HIGHEST
        )
        return reduce_over(forward_summed.reshape(RB_DEV * block_edge, responses), "feat", n_feat)

    def slab_of(current):
        return lax.all_gather(current.astype(jnp.bfloat16), "feat", axis=0, tiled=True)

    def gradient_rows(current):
        return reduce_over(backward(slab_of(current)), "comp", n_comp)

    def own_part(full):
        return lax.dynamic_slice_in_dim(full, comp_index * own_rows, own_rows, axis=0)

    def col_sq(x):
        return jnp.sum(x * x, axis=0)

    residual = right_side

    gradient_own = gradient_rows(residual)
    direction = lax.all_gather(gradient_own, "comp", axis=0, tiled=True)
    image_rows = forward(direction)
    energy, image_energy = total_over_mesh(
        jnp.stack([col_sq(gradient_own), col_sq(image_rows)]), n_comp, n_feat
    )
    step_size = energy / (image_energy + ridge * energy)
    solution = step_size * direction
    residual = residual - step_size * image_rows

    for _ in range(1, ITERS):
        gradient_own = gradient_rows(residual) - ridge * own_part(solution)
        gathered = lax.all_gather(
            jnp.concatenate([gradient_own, col_sq(gradient_own)[None]], axis=0),
            "comp",
            axis=0,
            tiled=False,
        )
        gradient = gathered[:, :own_rows].reshape(feat_rows, responses)
        comp_energy = jnp.sum(gathered[:, own_rows], axis=0)
        spread = jnp.broadcast_to(comp_energy[None, None], (n_feat, 1, responses))
        next_energy = lax.all_to_all(spread, "feat", 0, 0, tiled=True).sum(0)[0]
        direction = gradient + next_energy / energy * direction
        energy = next_energy
        image_rows = forward(direction)
        image_energy, direction_energy = total_over_mesh(
            jnp.stack([col_sq(image_rows), col_sq(own_part(direction))]), n_comp, n_feat
        )
        step_size = energy / (image_energy + ridge * direction_energy)
        solution = solution + step_size * direction
        residual = residual - step_size * image_rows
    return (solution, residual)


def solution(mesh):
    placed = (
        P("comp", "feat", None, None, None),
        P("comp", "feat", None),
        P("comp", "feat", None),
        P("comp", "feat"),
        P(("comp", "feat"), None),
        P(),
    )
    n_comp = mesh.shape["comp"]
    n_feat = mesh.shape["feat"]

    def body(*args):
        return shards(*args, n_comp=n_comp, n_feat=n_feat)

    return jax.shard_map(
        body,
        mesh=mesh,
        in_specs=placed,
        out_specs=(P("feat", None), P(("comp", "feat"), None)),
        check_vma=False,
    )
```

```python
import jax
import jax.numpy as jnp
from jax import lax
from jax.sharding import PartitionSpec as P

RB_DEV = 16
CB_DEV = 14
ITERS = 2


def reduce_over(partial, axis, parts):
    rows = partial.shape[0] // parts
    pieces = partial.reshape(parts, rows, *partial.shape[1:])
    return lax.all_to_all(pieces, axis, 0, 0, tiled=True).sum(0)


def total_over_mesh(stacked, n_comp, n_feat):
    spread = jnp.broadcast_to(stacked[None], (n_feat,) + stacked.shape)
    by_feat = lax.all_to_all(spread, "feat", 0, 0, tiled=True).sum(0)
    spread = jnp.broadcast_to(by_feat[None], (n_comp,) + stacked.shape)
    return lax.all_to_all(spread, "comp", 0, 0, tiled=True).sum(0)


def shards(block_values, block_rows, block_cols, block_counts, right_side, ridge, n_comp, n_feat):
    values = block_values[0, 0]
    slot_rows = block_rows[0, 0]
    slot_cols = block_cols[0, 0]
    count_of_slots = block_counts[0, 0]
    responses = right_side.shape[1]
    total_slot_number = values.shape[0]
    block_edge = values.shape[1]
    feat_rows = CB_DEV * block_edge
    own_rows = feat_rows // n_comp
    comp_index = lax.axis_index("comp")
    slot_live = (jnp.arange(total_slot_number) < count_of_slots).astype(jnp.float32)
    row_lookup_table = (jnp.arange(RB_DEV)[:, None] == slot_rows[None, :]).astype(
        jnp.float32
    ) * slot_live[None, :]
    col_table = (jnp.arange(CB_DEV)[:, None] == slot_cols[None, :]).astype(jnp.float32) * slot_live[
        None, :
    ]

    def backward(low_slab):
        row_slabs = low_slab.reshape(RB_DEV, block_edge, responses)
        selected = jnp.take(row_slabs, slot_rows, axis=0)
        block_products = jnp.einsum(
            "sij,sik->sjk", values, selected, preferred_element_type=jnp.float32
        )
        summed = jnp.einsum(
            "qs,sjk->qjk", col_table, block_products, precision=lax.Precision.HIGHEST
        )
        return summed.reshape(feat_rows, responses)

    def forward(direction):
        col_panels = direction.astype(jnp.bfloat16).reshape(CB_DEV, block_edge, responses)
        forward_selected = jnp.take(col_panels, slot_cols, axis=0)
        forward_block_products = jnp.einsum(
            "sij,sjk->sik", values, forward_selected, preferred_element_type=jnp.float32
        )
        forward_summed = jnp.einsum(
            "rs,sik->rik", row_lookup_table, forward_block_products, precision=lax.Precision.HIGHEST
        )
        return reduce_over(forward_summed.reshape(RB_DEV * block_edge, responses), "feat", n_feat)

    def slab_of(current):
        return lax.all_gather(current.astype(jnp.bfloat16), "feat", axis=0, tiled=True)

    core = comp_index % 2
    half_rows = feat_rows // 2
    part_rows = half_rows // n_comp
    siblings = [(i, i ^ 1) for i in range(n_comp)]

    def gradient_rows(current):
        partial = backward(slab_of(current))
        kept = lax.dynamic_slice_in_dim(partial, core * half_rows, half_rows, axis=0)
        sent = lax.dynamic_slice_in_dim(partial, (1 - core) * half_rows, half_rows, axis=0)
        chip_sum = kept + lax.ppermute(sent, "comp", siblings)
        pieces = chip_sum.reshape(n_comp, part_rows, chip_sum.shape[1])
        landed = lax.all_to_all(pieces, "comp", 0, 0, tiled=True)
        halves = landed.reshape(n_comp // 2, 2, part_rows, chip_sum.shape[1]).sum(0)
        return halves.reshape(own_rows, chip_sum.shape[1])

    def whole_of(gathered):
        split = gathered.reshape(n_comp, 2, part_rows, gathered.shape[-1])
        return split.transpose(1, 0, 2, 3).reshape(feat_rows, gathered.shape[-1])

    def own_part(full):
        split = full.reshape(2, n_comp, part_rows, full.shape[-1])
        mine = lax.dynamic_slice_in_dim(split, comp_index, 1, axis=1)
        return mine.reshape(own_rows, full.shape[-1])

    def col_sq(x):
        return jnp.sum(x * x, axis=0)

    residual = right_side

    gradient_own = gradient_rows(residual)
    direction = whole_of(lax.all_gather(gradient_own, "comp", axis=0, tiled=False))
    image_rows = forward(direction)
    energy, image_energy = total_over_mesh(
        jnp.stack([col_sq(gradient_own), col_sq(image_rows)]), n_comp, n_feat
    )
    step_size = energy / (image_energy + ridge * energy)
    solution = step_size * direction
    residual = residual - step_size * image_rows

    for _ in range(1, ITERS):
        gradient_own = gradient_rows(residual) - ridge * own_part(solution)
        gathered = lax.all_gather(
            jnp.concatenate([gradient_own, col_sq(gradient_own)[None]], axis=0),
            "comp",
            axis=0,
            tiled=False,
        )
        gradient = whole_of(gathered[:, :own_rows])
        comp_energy = jnp.sum(gathered[:, own_rows], axis=0)
        spread = jnp.broadcast_to(comp_energy[None, None], (n_feat, 1, responses))
        next_energy = lax.all_to_all(spread, "feat", 0, 0, tiled=True).sum(0)[0]
        direction = gradient + next_energy / energy * direction
        energy = next_energy
        image_rows = forward(direction)
        image_energy, direction_energy = total_over_mesh(
            jnp.stack([col_sq(image_rows), col_sq(own_part(direction))]), n_comp, n_feat
        )
        step_size = energy / (image_energy + ridge * direction_energy)
        solution = solution + step_size * direction
        residual = residual - step_size * image_rows
    return (solution, residual)


def solution(mesh):
    placed = (
        P("comp", "feat", None, None, None),
        P("comp", "feat", None),
        P("comp", "feat", None),
        P("comp", "feat"),
        P(("comp", "feat"), None),
        P(),
    )
    n_comp = mesh.shape["comp"]
    n_feat = mesh.shape["feat"]

    def body(*args):
        return shards(*args, n_comp=n_comp, n_feat=n_feat)

    return jax.shard_map(
        body,
        mesh=mesh,
        in_specs=placed,
        out_specs=(P("feat", None), P(("comp", "feat"), None)),
        check_vma=False,
    )
```

```python
import functools

import jax
import jax.numpy as jnp
from jax import lax
from jax.experimental import pallas as pl
from jax.experimental.pallas import tpu as pltpu
from jax.sharding import PartitionSpec as P

RB_DEV = 16
CB_DEV = 14
ITERS = 2


def _block_kernel(transpose, count_ref, out_idx_ref, in_idx_ref, values_ref, x_ref, out_ref):
    edge = values_ref.shape[1]
    out_ref[...] = jnp.zeros_like(out_ref)

    def body(s, carry):
        @pl.when(s < count_ref[0])
        def _():
            src = pl.multiple_of(in_idx_ref[s] * edge, edge)
            dst = pl.multiple_of(out_idx_ref[s] * edge, edge)
            block = values_ref[s]
            x = x_ref[pl.ds(src, edge), :]
            if transpose:
                prod = lax.dot_general(
                    block, x, (((0,), (0,)), ((), ())), preferred_element_type=jnp.float32
                )
            else:
                prod = jnp.dot(block, x, preferred_element_type=jnp.float32)
            out_ref[pl.ds(dst, edge), :] += prod

        return carry

    lax.fori_loop(0, values_ref.shape[0], body, 0)


def block_apply(values, count, out_idx, in_idx, x, out_blocks, transpose):
    edge = values.shape[1]
    smem = pl.BlockSpec(memory_space=pltpu.SMEM)
    vmem = pl.BlockSpec(memory_space=pltpu.VMEM)
    return pl.pallas_call(
        functools.partial(_block_kernel, transpose),
        out_shape=jax.ShapeDtypeStruct((out_blocks * edge, x.shape[1]), jnp.float32),
        in_specs=[smem, smem, smem, vmem, vmem],
        out_specs=vmem,
    )(count.reshape(1), out_idx, in_idx, values, x)


def reduce_over(partial, axis, parts):
    rows = partial.shape[0] // parts
    pieces = partial.reshape(parts, rows, *partial.shape[1:])
    return lax.all_to_all(pieces, axis, 0, 0, tiled=True).sum(0)


def total_over_mesh(stacked, n_comp, n_feat):
    spread = jnp.broadcast_to(stacked[None], (n_feat,) + stacked.shape)
    by_feat = lax.all_to_all(spread, "feat", 0, 0, tiled=True).sum(0)
    spread = jnp.broadcast_to(by_feat[None], (n_comp,) + stacked.shape)
    return lax.all_to_all(spread, "comp", 0, 0, tiled=True).sum(0)


def shards(block_values, block_rows, block_cols, block_counts, right_side, ridge, n_comp, n_feat):
    values = block_values[0, 0]
    slot_rows = block_rows[0, 0]
    slot_cols = block_cols[0, 0]
    count_of_slots = block_counts[0, 0]
    responses = right_side.shape[1]
    block_edge = values.shape[1]
    feat_rows = CB_DEV * block_edge
    own_rows = feat_rows // n_comp
    comp_index = lax.axis_index("comp")

    def backward(low_slab):
        return block_apply(values, count_of_slots, slot_cols, slot_rows, low_slab, CB_DEV, True)

    def forward(direction):
        low = direction.astype(jnp.bfloat16)
        summed = block_apply(values, count_of_slots, slot_rows, slot_cols, low, RB_DEV, False)
        return reduce_over(summed, "feat", n_feat)

    def slab_of(current):
        return lax.all_gather(current.astype(jnp.bfloat16), "feat", axis=0, tiled=True)

    core = comp_index % 2
    half_rows = feat_rows // 2
    part_rows = half_rows // n_comp
    siblings = [(i, i ^ 1) for i in range(n_comp)]

    def gradient_rows(current):
        partial = backward(slab_of(current))
        kept = lax.dynamic_slice_in_dim(partial, core * half_rows, half_rows, axis=0)
        sent = lax.dynamic_slice_in_dim(partial, (1 - core) * half_rows, half_rows, axis=0)
        chip_sum = kept + lax.ppermute(sent, "comp", siblings)
        pieces = chip_sum.reshape(n_comp, part_rows, chip_sum.shape[1])
        landed = lax.all_to_all(pieces, "comp", 0, 0, tiled=True)
        halves = landed.reshape(n_comp // 2, 2, part_rows, chip_sum.shape[1]).sum(0)
        return halves.reshape(own_rows, chip_sum.shape[1])

    def whole_of(gathered):
        split = gathered.reshape(n_comp, 2, part_rows, gathered.shape[-1])
        return split.transpose(1, 0, 2, 3).reshape(feat_rows, gathered.shape[-1])

    def own_part(full):
        split = full.reshape(2, n_comp, part_rows, full.shape[-1])
        mine = lax.dynamic_slice_in_dim(split, comp_index, 1, axis=1)
        return mine.reshape(own_rows, full.shape[-1])

    def col_sq(x):
        return jnp.sum(x * x, axis=0)

    residual = right_side

    gradient_own = gradient_rows(residual)
    direction = whole_of(lax.all_gather(gradient_own, "comp", axis=0, tiled=False))
    image_rows = forward(direction)
    energy, image_energy = total_over_mesh(
        jnp.stack([col_sq(gradient_own), col_sq(image_rows)]), n_comp, n_feat
    )
    step_size = energy / (image_energy + ridge * energy)
    solution = step_size * direction
    residual = residual - step_size * image_rows

    for _ in range(1, ITERS):
        gradient_own = gradient_rows(residual) - ridge * own_part(solution)
        gathered = lax.all_gather(
            jnp.concatenate([gradient_own, col_sq(gradient_own)[None]], axis=0),
            "comp",
            axis=0,
            tiled=False,
        )
        gradient = whole_of(gathered[:, :own_rows])
        comp_energy = jnp.sum(gathered[:, own_rows], axis=0)
        spread = jnp.broadcast_to(comp_energy[None, None], (n_feat, 1, responses))
        next_energy = lax.all_to_all(spread, "feat", 0, 0, tiled=True).sum(0)[0]
        direction = gradient + next_energy / energy * direction
        energy = next_energy
        image_rows = forward(direction)
        image_energy, direction_energy = total_over_mesh(
            jnp.stack([col_sq(image_rows), col_sq(own_part(direction))]), n_comp, n_feat
        )
        step_size = energy / (image_energy + ridge * direction_energy)
        solution = solution + step_size * direction
        residual = residual - step_size * image_rows
    return (solution, residual)


def solution(mesh):
    placed = (
        P("comp", "feat", None, None, None),
        P("comp", "feat", None),
        P("comp", "feat", None),
        P("comp", "feat"),
        P(("comp", "feat"), None),
        P(),
    )
    n_comp = mesh.shape["comp"]
    n_feat = mesh.shape["feat"]

    def body(*args):
        return shards(*args, n_comp=n_comp, n_feat=n_feat)

    return jax.shard_map(
        body,
        mesh=mesh,
        in_specs=placed,
        out_specs=(P("feat", None), P(("comp", "feat"), None)),
        check_vma=False,
    )
```

```python
import functools

import jax
import jax.numpy as jnp
from jax import lax
from jax.experimental import pallas as pl
from jax.experimental.pallas import tpu as pltpu
from jax.sharding import PartitionSpec as P

RB_DEV = 16
CB_DEV = 14
ITERS = 2


def _block_kernel(transpose, count_ref, out_idx_ref, in_idx_ref, values_ref, x_ref, out_ref):
    edge = values_ref.shape[1]
    out_ref[...] = jnp.zeros_like(out_ref)

    def body(s, carry):
        @pl.when(s < count_ref[0])
        def _():
            src = pl.multiple_of(in_idx_ref[s] * edge, edge)
            dst = pl.multiple_of(out_idx_ref[s] * edge, edge)
            block = values_ref[s]
            x = x_ref[pl.ds(src, edge), :]
            if transpose:
                prod = lax.dot_general(
                    block, x, (((0,), (0,)), ((), ())), preferred_element_type=jnp.float32
                )
            else:
                prod = jnp.dot(block, x, preferred_element_type=jnp.float32)
            out_ref[pl.ds(dst, edge), :] += prod

        return carry

    lax.fori_loop(0, values_ref.shape[0], body, 0)


def block_apply(values, count, out_idx, in_idx, x, out_blocks, transpose):
    edge = values.shape[1]
    smem = pl.BlockSpec(memory_space=pltpu.SMEM)
    vmem = pl.BlockSpec(memory_space=pltpu.VMEM)
    return pl.pallas_call(
        functools.partial(_block_kernel, transpose),
        out_shape=jax.ShapeDtypeStruct((out_blocks * edge, x.shape[1]), jnp.float32),
        in_specs=[smem, smem, smem, vmem, vmem],
        out_specs=vmem,
    )(count.reshape(1), out_idx, in_idx, values, x)


def reduce_over(partial, axis, parts):
    rows = partial.shape[0] // parts
    pieces = partial.reshape(parts, rows, *partial.shape[1:])
    return lax.all_to_all(pieces, axis, 0, 0, tiled=True).sum(0)


def total_over_mesh(stacked, n_comp, n_feat):
    spread = jnp.broadcast_to(stacked[None], (n_feat,) + stacked.shape)
    by_feat = lax.all_to_all(spread, "feat", 0, 0, tiled=True).sum(0)
    spread = jnp.broadcast_to(by_feat[None], (n_comp,) + stacked.shape)
    return lax.all_to_all(spread, "comp", 0, 0, tiled=True).sum(0)


def shards(block_values, block_rows, block_cols, block_counts, right_side, ridge, n_comp, n_feat):
    values = block_values[0, 0]
    slot_rows = block_rows[0, 0]
    slot_cols = block_cols[0, 0]
    count_of_slots = block_counts[0, 0]
    responses = right_side.shape[1]
    block_edge = values.shape[1]
    feat_rows = CB_DEV * block_edge
    own_rows = feat_rows // n_comp
    comp_index = lax.axis_index("comp")

    def backward(low_slab):
        return block_apply(values, count_of_slots, slot_cols, slot_rows, low_slab, CB_DEV, True)

    def forward(direction):
        low = direction.astype(jnp.bfloat16)
        summed = block_apply(values, count_of_slots, slot_rows, slot_cols, low, RB_DEV, False)
        return reduce_over(summed, "feat", n_feat)

    core = comp_index % 2
    half_rows = feat_rows // 2
    part_rows = half_rows // n_comp
    siblings = [(i, i ^ 1) for i in range(n_comp)]

    def reduce_gradient(partial):
        kept = lax.dynamic_slice_in_dim(partial, core * half_rows, half_rows, axis=0)
        sent = lax.dynamic_slice_in_dim(partial, (1 - core) * half_rows, half_rows, axis=0)
        chip_sum = kept + lax.ppermute(sent, "comp", siblings)
        pieces = chip_sum.reshape(n_comp, part_rows, chip_sum.shape[1])
        landed = lax.all_to_all(pieces, "comp", 0, 0, tiled=True)
        halves = landed.reshape(n_comp // 2, 2, part_rows, chip_sum.shape[1]).sum(0)
        return halves.reshape(own_rows, chip_sum.shape[1])

    def whole_of(gathered):
        split = gathered.reshape(n_comp, 2, part_rows, gathered.shape[-1])
        return split.transpose(1, 0, 2, 3).reshape(feat_rows, gathered.shape[-1])

    def own_part(full):
        split = full.reshape(2, n_comp, part_rows, full.shape[-1])
        mine = lax.dynamic_slice_in_dim(split, comp_index, 1, axis=1)
        return mine.reshape(own_rows, full.shape[-1])

    def col_sq(x):
        return jnp.sum(x * x, axis=0)

    feat_index = lax.axis_index("feat")

    def gather_feat(own):
        spread = jnp.broadcast_to(own[None], (n_feat,) + own.shape)
        return lax.all_to_all(spread, "feat", 0, 0, tiled=True)

    def comp_total(stacked):
        spread = jnp.broadcast_to(stacked[None], (n_comp,) + stacked.shape)
        return lax.all_to_all(spread, "comp", 0, 0, tiled=True).sum(0)

    own_block = right_side.shape[0]
    residual_slab = gather_feat(right_side).reshape(RB_DEV * own_block, responses)

    def low_slab(slab):
        return slab.astype(jnp.bfloat16)

    gradient_own = reduce_gradient(backward(low_slab(residual_slab)))
    energy_own = col_sq(gradient_own)
    direction = whole_of(lax.all_gather(gradient_own, "comp", axis=0, tiled=False))
    energy = None
    solution = None
    for step_index in range(ITERS):
        last = step_index + 1 == ITERS
        if step_index > 0:
            gradient_own = reduce_gradient(backward(low_slab(residual_slab))) - ridge * own_part(
                solution
            )
            gathered = lax.all_gather(
                jnp.concatenate([gradient_own, col_sq(gradient_own)[None]], axis=0),
                "comp",
                axis=0,
                tiled=False,
            )
            gradient = whole_of(gathered[:, :own_rows])
            comp_energy = jnp.sum(gathered[:, own_rows], axis=0)
            spread = jnp.broadcast_to(comp_energy[None, None], (n_feat, 1, responses))
            next_energy = lax.all_to_all(spread, "feat", 0, 0, tiled=True).sum(0)[0]
            direction = gradient + next_energy / energy * direction
            energy = next_energy
        image_rows = forward(direction)
        if last:
            sums = [col_sq(image_rows), col_sq(own_part(direction))]
            if energy is None:
                sums.append(energy_own)
            totals = total_over_mesh(jnp.stack(sums), n_comp, n_feat)
            if energy is None:
                energy = totals[2]
            image_energy, direction_energy = totals[0], totals[1]
        else:
            parts = [image_rows, col_sq(own_part(direction))[None]]
            if energy is None:
                parts.append(energy_own[None])
            gathered = gather_feat(jnp.concatenate(parts, axis=0))
            image_slab = gathered[:, :own_block].reshape(RB_DEV * own_block, responses)
            feat_sums = jnp.sum(gathered[:, own_block:], axis=0)
            totals = comp_total(jnp.concatenate([col_sq(image_slab)[None], feat_sums], axis=0))
            if energy is None:
                energy = totals[2]
            image_energy, direction_energy = totals[0], totals[1]
        step_size = energy / (image_energy + ridge * direction_energy)
        solution = step_size * direction if solution is None else solution + step_size * direction
        if last:
            own_residual = lax.dynamic_slice_in_dim(residual_slab, feat_index * own_block, own_block)
            residual = own_residual - step_size * image_rows
        else:
            residual_slab = residual_slab - step_size * image_slab
    return (solution, residual)


def solution(mesh):
    placed = (
        P("comp", "feat", None, None, None),
        P("comp", "feat", None),
        P("comp", "feat", None),
        P("comp", "feat"),
        P(("comp", "feat"), None),
        P(),
    )
    n_comp = mesh.shape["comp"]
    n_feat = mesh.shape["feat"]

    def body(*args):
        return shards(*args, n_comp=n_comp, n_feat=n_feat)

    return jax.shard_map(
        body,
        mesh=mesh,
        in_specs=placed,
        out_specs=(P("feat", None), P(("comp", "feat"), None)),
        check_vma=False,
    )
```

```python
import functools

import jax
import jax.numpy as jnp
from jax import lax
from jax.experimental import pallas as pl
from jax.experimental.pallas import tpu as pltpu
from jax.sharding import PartitionSpec as P

RB_DEV = 16
CB_DEV = 14
ITERS = 2


def _block_kernel(transpose, count_ref, out_idx_ref, in_idx_ref, values_ref, x_ref, out_ref):
    edge = values_ref.shape[1]
    out_ref[...] = jnp.zeros_like(out_ref)

    def body(s, carry):
        @pl.when(s < count_ref[0])
        def _():
            src = pl.multiple_of(in_idx_ref[s] * edge, edge)
            dst = pl.multiple_of(out_idx_ref[s] * edge, edge)
            block = values_ref[s]
            x = x_ref[pl.ds(src, edge), :]
            if transpose:
                prod = lax.dot_general(
                    block, x, (((0,), (0,)), ((), ())), preferred_element_type=jnp.float32
                )
            else:
                prod = jnp.dot(block, x, preferred_element_type=jnp.float32)
            out_ref[pl.ds(dst, edge), :] += prod

        return carry

    lax.fori_loop(0, values_ref.shape[0], body, 0)


def block_apply(values, count, out_idx, in_idx, x, out_blocks, transpose):
    edge = values.shape[1]
    smem = pl.BlockSpec(memory_space=pltpu.SMEM)
    vmem = pl.BlockSpec(memory_space=pltpu.VMEM)
    return pl.pallas_call(
        functools.partial(_block_kernel, transpose),
        out_shape=jax.ShapeDtypeStruct((out_blocks * edge, x.shape[1]), jnp.float32),
        in_specs=[smem, smem, smem, vmem, vmem],
        out_specs=vmem,
    )(count.reshape(1), out_idx, in_idx, values, x)


def reduce_over(partial, axis, parts):
    rows = partial.shape[0] // parts
    pieces = partial.reshape(parts, rows, *partial.shape[1:])
    return lax.all_to_all(pieces, axis, 0, 0, tiled=True).sum(0)


def shards(block_values, block_rows, block_cols, block_counts, right_side, ridge, n_comp, n_feat):
    values = block_values[0, 0]
    slot_rows = block_rows[0, 0]
    slot_cols = block_cols[0, 0]
    count_of_slots = block_counts[0, 0]
    responses = right_side.shape[1]
    block_edge = values.shape[1]
    feat_rows = CB_DEV * block_edge
    own_rows = feat_rows // n_comp
    comp_index = lax.axis_index("comp")

    def backward(low_slab):
        return block_apply(values, count_of_slots, slot_cols, slot_rows, low_slab, CB_DEV, True)

    def forward(direction):
        low = direction.astype(jnp.bfloat16)
        summed = block_apply(values, count_of_slots, slot_rows, slot_cols, low, RB_DEV, False)
        return reduce_over(summed, "feat", n_feat)

    core = comp_index % 2
    chip = comp_index // 2
    n_chips = n_comp // 2
    half_rows = feat_rows // 2
    siblings = [(i, i ^ 1) for i in range(n_comp)]
    same_core = [[i for i in range(n_comp) if i % 2 == p] for p in range(2)]

    def swap_with_sibling(x):
        return lax.ppermute(x, "comp", siblings)

    def reduce_gradient(partial):
        kept = lax.dynamic_slice_in_dim(partial, core * half_rows, half_rows, axis=0)
        sent = lax.dynamic_slice_in_dim(partial, (1 - core) * half_rows, half_rows, axis=0)
        chip_sum = kept + swap_with_sibling(sent)
        pieces = chip_sum.reshape(n_chips, own_rows, chip_sum.shape[1])
        landed = lax.all_to_all(pieces, "comp", 0, 0, tiled=True, axis_index_groups=same_core)
        return landed.sum(0)

    def gather_gradient(own):
        got = lax.all_gather(own, "comp", axis=0, tiled=False, axis_index_groups=same_core)
        half = got[:, :own_rows].reshape(half_rows, own.shape[1])
        sums = jnp.sum(got[:, own_rows:], axis=0)
        other_half, other_sums = swap_with_sibling((half, sums))
        first = jnp.where(core == 0, half, other_half)
        second = jnp.where(core == 0, other_half, half)
        return jnp.concatenate([first, second], axis=0), sums + other_sums

    def own_part(full):
        return lax.dynamic_slice_in_dim(full, core * half_rows + chip * own_rows, own_rows, axis=0)

    def col_sq(x):
        return jnp.sum(x * x, axis=0)

    feat_index = lax.axis_index("feat")

    def gather_feat(own):
        spread = jnp.broadcast_to(own[None], (n_feat,) + own.shape)
        return lax.all_to_all(spread, "feat", 0, 0, tiled=True)

    def comp_total(stacked):
        spread = jnp.broadcast_to(stacked[None], (n_chips,) + stacked.shape)
        by_chip = lax.all_to_all(spread, "comp", 0, 0, tiled=True, axis_index_groups=same_core)
        mine = by_chip.sum(0)
        return mine + swap_with_sibling(mine)

    own_block = right_side.shape[0]
    residual_slab = gather_feat(right_side).reshape(RB_DEV * own_block, responses)

    def low_slab(slab):
        return slab.astype(jnp.bfloat16)

    gradient_own = reduce_gradient(backward(low_slab(residual_slab)))
    energy_own = col_sq(gradient_own)
    direction, _ = gather_gradient(gradient_own)
    energy = None
    solution = None
    for step_index in range(ITERS):
        last = step_index + 1 == ITERS
        if step_index > 0:
            gradient_own = reduce_gradient(backward(low_slab(residual_slab))) - ridge * own_part(
                solution
            )
            gradient, comp_energy = gather_gradient(
                jnp.concatenate([gradient_own, col_sq(gradient_own)[None]], axis=0)
            )
            comp_energy = comp_energy[0]
            spread = jnp.broadcast_to(comp_energy[None, None], (n_feat, 1, responses))
            next_energy = lax.all_to_all(spread, "feat", 0, 0, tiled=True).sum(0)[0]
            direction = gradient + next_energy / energy * direction
            energy = next_energy
        image_rows = forward(direction)
        if last:
            sums = [col_sq(image_rows), col_sq(own_part(direction))]
            if energy is None:
                sums.append(energy_own)
            spread = jnp.broadcast_to(jnp.stack(sums)[None], (n_feat, len(sums), responses))
            totals = comp_total(lax.all_to_all(spread, "feat", 0, 0, tiled=True).sum(0))
            if energy is None:
                energy = totals[2]
            image_energy, direction_energy = totals[0], totals[1]
        else:
            parts = [image_rows, col_sq(own_part(direction))[None]]
            if energy is None:
                parts.append(energy_own[None])
            gathered = gather_feat(jnp.concatenate(parts, axis=0))
            image_slab = gathered[:, :own_block].reshape(RB_DEV * own_block, responses)
            feat_sums = jnp.sum(gathered[:, own_block:], axis=0)
            totals = comp_total(jnp.concatenate([col_sq(image_slab)[None], feat_sums], axis=0))
            if energy is None:
                energy = totals[2]
            image_energy, direction_energy = totals[0], totals[1]
        step_size = energy / (image_energy + ridge * direction_energy)
        solution = step_size * direction if solution is None else solution + step_size * direction
        if last:
            own_residual = lax.dynamic_slice_in_dim(residual_slab, feat_index * own_block, own_block)
            residual = own_residual - step_size * image_rows
        else:
            residual_slab = residual_slab - step_size * image_slab
    return (solution, residual)


def solution(mesh):
    placed = (
        P("comp", "feat", None, None, None),
        P("comp", "feat", None),
        P("comp", "feat", None),
        P("comp", "feat"),
        P(("comp", "feat"), None),
        P(),
    )
    n_comp = mesh.shape["comp"]
    n_feat = mesh.shape["feat"]

    def body(*args):
        return shards(*args, n_comp=n_comp, n_feat=n_feat)

    return jax.shard_map(
        body,
        mesh=mesh,
        in_specs=placed,
        out_specs=(P("feat", None), P(("comp", "feat"), None)),
        check_vma=False,
    )
```

```python
import functools

import jax
import jax.numpy as jnp
from jax import lax
from jax.experimental import pallas as pl
from jax.experimental.pallas import tpu as pltpu
from jax.sharding import PartitionSpec as P

RB_DEV = 16
CB_DEV = 14
ITERS = 2


def _block_kernel(transpose, count_ref, out_idx_ref, in_idx_ref, values_ref, x_ref, out_ref):
    edge = values_ref.shape[1]
    out_ref[...] = jnp.zeros_like(out_ref)

    def body(s, carry):
        @pl.when(s < count_ref[0])
        def _():
            src = pl.multiple_of(in_idx_ref[s] * edge, edge)
            dst = pl.multiple_of(out_idx_ref[s] * edge, edge)
            block = values_ref[s]
            x = x_ref[pl.ds(src, edge), :]
            if transpose:
                prod = lax.dot_general(
                    block, x, (((0,), (0,)), ((), ())), preferred_element_type=jnp.float32
                )
            else:
                prod = jnp.dot(block, x, preferred_element_type=jnp.float32)
            out_ref[pl.ds(dst, edge), :] += prod

        return carry

    lax.fori_loop(0, values_ref.shape[0], body, 0)


def block_apply(values, count, out_idx, in_idx, x, out_blocks, transpose):
    edge = values.shape[1]
    smem = pl.BlockSpec(memory_space=pltpu.SMEM)
    vmem = pl.BlockSpec(memory_space=pltpu.VMEM)
    return pl.pallas_call(
        functools.partial(_block_kernel, transpose),
        out_shape=jax.ShapeDtypeStruct((out_blocks * edge, x.shape[1]), jnp.float32),
        in_specs=[smem, smem, smem, vmem, vmem],
        out_specs=vmem,
    )(count.reshape(1), out_idx, in_idx, values, x)


def reduce_over(partial, axis, parts):
    rows = partial.shape[0] // parts
    pieces = partial.reshape(parts, rows, *partial.shape[1:])
    return lax.all_to_all(pieces, axis, 0, 0, tiled=True).sum(0)


def shards(block_values, block_rows, block_cols, block_counts, right_side, ridge, n_comp, n_feat):
    values = block_values[0, 0]
    slot_rows = block_rows[0, 0]
    slot_cols = block_cols[0, 0]
    count_of_slots = block_counts[0, 0]
    responses = right_side.shape[1]
    block_edge = values.shape[1]
    feat_rows = CB_DEV * block_edge
    own_rows = feat_rows // n_comp
    comp_index = lax.axis_index("comp")

    def backward(low_slab):
        return block_apply(values, count_of_slots, slot_cols, slot_rows, low_slab, CB_DEV, True)

    def forward(direction):
        low = direction.astype(jnp.bfloat16)
        summed = block_apply(values, count_of_slots, slot_rows, slot_cols, low, RB_DEV, False)
        return reduce_over(summed, "feat", n_feat)

    core = comp_index % 2
    chip = comp_index // 2
    n_chips = n_comp // 2
    half_rows = feat_rows // 2
    siblings = [(i, i ^ 1) for i in range(n_comp)]
    same_core = [[i for i in range(n_comp) if i % 2 == p] for p in range(2)]

    def swap_with_sibling(x):
        return lax.ppermute(x, "comp", siblings)

    def reduce_gradient(partial):
        kept = lax.dynamic_slice_in_dim(partial, core * half_rows, half_rows, axis=0)
        sent = lax.dynamic_slice_in_dim(partial, (1 - core) * half_rows, half_rows, axis=0)
        chip_sum = kept + swap_with_sibling(sent)
        pieces = chip_sum.reshape(n_chips, own_rows, chip_sum.shape[1])
        landed = lax.all_to_all(pieces, "comp", 0, 0, tiled=True, axis_index_groups=same_core)
        return landed.sum(0)

    def gather_gradient(own):
        got = lax.all_gather(own, "comp", axis=0, tiled=False)
        by_chip = got[:, :own_rows].reshape(n_chips, 2, own_rows, own.shape[1])
        rows = by_chip.transpose(1, 0, 2, 3).reshape(feat_rows, own.shape[1])
        return rows, jnp.sum(got[:, own_rows:], axis=0)

    def own_part(full):
        return lax.dynamic_slice_in_dim(full, core * half_rows + chip * own_rows, own_rows, axis=0)

    def col_sq(x):
        return jnp.sum(x * x, axis=0)

    feat_index = lax.axis_index("feat")

    def gather_feat(own):
        spread = jnp.broadcast_to(own[None], (n_feat,) + own.shape)
        return lax.all_to_all(spread, "feat", 0, 0, tiled=True)

    def comp_total(stacked):
        spread = jnp.broadcast_to(stacked[None], (n_comp,) + stacked.shape)
        return lax.all_to_all(spread, "comp", 0, 0, tiled=True).sum(0)

    own_block = right_side.shape[0]
    residual_slab = gather_feat(right_side).reshape(RB_DEV * own_block, responses)

    def low_slab(slab):
        return slab.astype(jnp.bfloat16)

    gradient_own = reduce_gradient(backward(low_slab(residual_slab)))
    energy_own = col_sq(gradient_own)
    direction, _ = gather_gradient(gradient_own)
    energy = None
    solution = None
    for step_index in range(ITERS):
        last = step_index + 1 == ITERS
        if step_index > 0:
            gradient_own = reduce_gradient(backward(low_slab(residual_slab))) - ridge * own_part(
                solution
            )
            gradient, comp_energy = gather_gradient(
                jnp.concatenate([gradient_own, col_sq(gradient_own)[None]], axis=0)
            )
            comp_energy = comp_energy[0]
            spread = jnp.broadcast_to(comp_energy[None, None], (n_feat, 1, responses))
            next_energy = lax.all_to_all(spread, "feat", 0, 0, tiled=True).sum(0)[0]
            direction = gradient + next_energy / energy * direction
            energy = next_energy
        image_rows = forward(direction)
        if last:
            sums = [col_sq(image_rows), col_sq(own_part(direction))]
            if energy is None:
                sums.append(energy_own)
            spread = jnp.broadcast_to(jnp.stack(sums)[None], (n_feat, len(sums), responses))
            totals = comp_total(lax.all_to_all(spread, "feat", 0, 0, tiled=True).sum(0))
            if energy is None:
                energy = totals[2]
            image_energy, direction_energy = totals[0], totals[1]
        else:
            parts = [image_rows, col_sq(own_part(direction))[None]]
            if energy is None:
                parts.append(energy_own[None])
            gathered = gather_feat(jnp.concatenate(parts, axis=0))
            image_slab = gathered[:, :own_block].reshape(RB_DEV * own_block, responses)
            feat_sums = jnp.sum(gathered[:, own_block:], axis=0)
            totals = comp_total(jnp.concatenate([col_sq(image_slab)[None], feat_sums], axis=0))
            if energy is None:
                energy = totals[2]
            image_energy, direction_energy = totals[0], totals[1]
        step_size = energy / (image_energy + ridge * direction_energy)
        solution = step_size * direction if solution is None else solution + step_size * direction
        if last:
            own_residual = lax.dynamic_slice_in_dim(residual_slab, feat_index * own_block, own_block)
            residual = own_residual - step_size * image_rows
        else:
            residual_slab = residual_slab - step_size * image_slab
    return (solution, residual)


def solution(mesh):
    placed = (
        P("comp", "feat", None, None, None),
        P("comp", "feat", None),
        P("comp", "feat", None),
        P("comp", "feat"),
        P(("comp", "feat"), None),
        P(),
    )
    n_comp = mesh.shape["comp"]
    n_feat = mesh.shape["feat"]

    def body(*args):
        return shards(*args, n_comp=n_comp, n_feat=n_feat)

    return jax.shard_map(
        body,
        mesh=mesh,
        in_specs=placed,
        out_specs=(P("feat", None), P(("comp", "feat"), None)),
        check_vma=False,
    )
```

```python
import functools

import jax
import jax.numpy as jnp
from jax import lax
from jax.experimental import pallas as pl
from jax.experimental.pallas import tpu as pltpu
from jax.sharding import PartitionSpec as P

RB_DEV = 16
CB_DEV = 14
ITERS = 2


def _block_kernel(transpose, count_ref, out_idx_ref, in_idx_ref, values_ref, x_ref, out_ref):
    edge = values_ref.shape[1]
    out_ref[...] = jnp.zeros_like(out_ref)

    def body(s, carry):
        @pl.when(s < count_ref[0])
        def _():
            src = pl.multiple_of(in_idx_ref[s] * edge, edge)
            dst = pl.multiple_of(out_idx_ref[s] * edge, edge)
            block = values_ref[s]
            x = x_ref[pl.ds(src, edge), :]
            if transpose:
                prod = lax.dot_general(
                    block, x, (((0,), (0,)), ((), ())), preferred_element_type=jnp.float32
                )
            else:
                prod = jnp.dot(block, x, preferred_element_type=jnp.float32)
            out_ref[pl.ds(dst, edge), :] += prod

        return carry

    lax.fori_loop(0, values_ref.shape[0], body, 0, unroll=True)


def block_apply(values, count, out_idx, in_idx, x, out_blocks, transpose):
    edge = values.shape[1]
    smem = pl.BlockSpec(memory_space=pltpu.SMEM)
    vmem = pl.BlockSpec(memory_space=pltpu.VMEM)
    return pl.pallas_call(
        functools.partial(_block_kernel, transpose),
        out_shape=jax.ShapeDtypeStruct((out_blocks * edge, x.shape[1]), jnp.float32),
        in_specs=[smem, smem, smem, vmem, vmem],
        out_specs=vmem,
    )(count.reshape(1), out_idx, in_idx, values, x)


def reduce_over(partial, axis, parts):
    rows = partial.shape[0] // parts
    pieces = partial.reshape(parts, rows, *partial.shape[1:])
    return lax.all_to_all(pieces, axis, 0, 0, tiled=True).sum(0)


def shards(block_values, block_rows, block_cols, block_counts, right_side, ridge, n_comp, n_feat):
    values = block_values[0, 0]
    slot_rows = block_rows[0, 0]
    slot_cols = block_cols[0, 0]
    count_of_slots = block_counts[0, 0]
    responses = right_side.shape[1]
    block_edge = values.shape[1]
    feat_rows = CB_DEV * block_edge
    own_rows = feat_rows // n_comp
    comp_index = lax.axis_index("comp")

    def backward(low_slab):
        return block_apply(values, count_of_slots, slot_cols, slot_rows, low_slab, CB_DEV, True)

    def forward(direction):
        low = direction.astype(jnp.bfloat16)
        summed = block_apply(values, count_of_slots, slot_rows, slot_cols, low, RB_DEV, False)
        return reduce_over(summed, "feat", n_feat)

    core = comp_index % 2
    chip = comp_index // 2
    n_chips = n_comp // 2
    half_rows = feat_rows // 2
    siblings = [(i, i ^ 1) for i in range(n_comp)]
    same_core = [[i for i in range(n_comp) if i % 2 == p] for p in range(2)]

    def swap_with_sibling(x):
        return lax.ppermute(x, "comp", siblings)

    def reduce_gradient(partial):
        kept = lax.dynamic_slice_in_dim(partial, core * half_rows, half_rows, axis=0)
        sent = lax.dynamic_slice_in_dim(partial, (1 - core) * half_rows, half_rows, axis=0)
        chip_sum = kept + swap_with_sibling(sent)
        pieces = chip_sum.reshape(n_chips, own_rows, chip_sum.shape[1])
        landed = lax.all_to_all(pieces, "comp", 0, 0, tiled=True, axis_index_groups=same_core)
        return landed.sum(0)

    def gather_gradient(own):
        got = lax.all_gather(own, "comp", axis=0, tiled=False)
        by_chip = got[:, :own_rows].reshape(n_chips, 2, own_rows, own.shape[1])
        rows = by_chip.transpose(1, 0, 2, 3).reshape(feat_rows, own.shape[1])
        return rows, jnp.sum(got[:, own_rows:], axis=0)

    def own_part(full):
        return lax.dynamic_slice_in_dim(full, core * half_rows + chip * own_rows, own_rows, axis=0)

    def col_sq(x):
        return jnp.sum(x * x, axis=0)

    feat_index = lax.axis_index("feat")

    def gather_feat(own):
        spread = jnp.broadcast_to(own[None], (n_feat,) + own.shape)
        return lax.all_to_all(spread, "feat", 0, 0, tiled=True)

    def comp_total(stacked):
        spread = jnp.broadcast_to(stacked[None], (n_comp,) + stacked.shape)
        return lax.all_to_all(spread, "comp", 0, 0, tiled=True).sum(0)

    own_block = right_side.shape[0]
    residual_slab = gather_feat(right_side).reshape(RB_DEV * own_block, responses)

    def low_slab(slab):
        return slab.astype(jnp.bfloat16)

    gradient_own = reduce_gradient(backward(low_slab(residual_slab)))
    energy_own = col_sq(gradient_own)
    direction, _ = gather_gradient(gradient_own)
    energy = None
    solution = None
    for step_index in range(ITERS):
        last = step_index + 1 == ITERS
        if step_index > 0:
            gradient_own = reduce_gradient(backward(low_slab(residual_slab))) - ridge * own_part(
                solution
            )
            gradient, comp_energy = gather_gradient(
                jnp.concatenate([gradient_own, col_sq(gradient_own)[None]], axis=0)
            )
            comp_energy = comp_energy[0]
            spread = jnp.broadcast_to(comp_energy[None, None], (n_feat, 1, responses))
            next_energy = lax.all_to_all(spread, "feat", 0, 0, tiled=True).sum(0)[0]
            direction = gradient + next_energy / energy * direction
            energy = next_energy
        image_rows = forward(direction)
        if last:
            sums = [col_sq(image_rows), col_sq(own_part(direction))]
            if energy is None:
                sums.append(energy_own)
            spread = jnp.broadcast_to(jnp.stack(sums)[None], (n_feat, len(sums), responses))
            totals = comp_total(lax.all_to_all(spread, "feat", 0, 0, tiled=True).sum(0))
            if energy is None:
                energy = totals[2]
            image_energy, direction_energy = totals[0], totals[1]
        else:
            parts = [image_rows, col_sq(own_part(direction))[None]]
            if energy is None:
                parts.append(energy_own[None])
            gathered = gather_feat(jnp.concatenate(parts, axis=0))
            image_slab = gathered[:, :own_block].reshape(RB_DEV * own_block, responses)
            feat_sums = jnp.sum(gathered[:, own_block:], axis=0)
            totals = comp_total(jnp.concatenate([col_sq(image_slab)[None], feat_sums], axis=0))
            if energy is None:
                energy = totals[2]
            image_energy, direction_energy = totals[0], totals[1]
        step_size = energy / (image_energy + ridge * direction_energy)
        solution = step_size * direction if solution is None else solution + step_size * direction
        if last:
            own_residual = lax.dynamic_slice_in_dim(residual_slab, feat_index * own_block, own_block)
            residual = own_residual - step_size * image_rows
        else:
            residual_slab = residual_slab - step_size * image_slab
    return (solution, residual)


def solution(mesh):
    placed = (
        P("comp", "feat", None, None, None),
        P("comp", "feat", None),
        P("comp", "feat", None),
        P("comp", "feat"),
        P(("comp", "feat"), None),
        P(),
    )
    n_comp = mesh.shape["comp"]
    n_feat = mesh.shape["feat"]

    def body(*args):
        return shards(*args, n_comp=n_comp, n_feat=n_feat)

    return jax.shard_map(
        body,
        mesh=mesh,
        in_specs=placed,
        out_specs=(P("feat", None), P(("comp", "feat"), None)),
        check_vma=False,
    )
```

```python
import functools

import jax
import jax.numpy as jnp
from jax import lax
from jax.experimental import pallas as pl
from jax.experimental.pallas import tpu as pltpu
from jax.sharding import PartitionSpec as P

RB_DEV = 16
CB_DEV = 14
ITERS = 2


def _block_kernel(transpose, count_ref, out_idx_ref, in_idx_ref, values_ref, x_ref, out_ref):
    edge = values_ref.shape[1]
    out_ref[...] = jnp.zeros_like(out_ref)

    def body(s, carry):
        @pl.when(s < count_ref[0])
        def _():
            src = pl.multiple_of(in_idx_ref[s] * edge, edge)
            dst = pl.multiple_of(out_idx_ref[s] * edge, edge)
            block = values_ref[s]
            x = x_ref[pl.ds(src, edge), :]
            if transpose:
                prod = lax.dot_general(
                    block, x, (((0,), (0,)), ((), ())), preferred_element_type=jnp.float32
                )
            else:
                prod = jnp.dot(block, x, preferred_element_type=jnp.float32)
            out_ref[pl.ds(dst, edge), :] += prod

        return carry

    lax.fori_loop(0, values_ref.shape[0], body, 0, unroll=True)


def block_apply(values, count, out_idx, in_idx, x, out_blocks, transpose):
    edge = values.shape[1]
    smem = pl.BlockSpec(memory_space=pltpu.SMEM)
    vmem = pl.BlockSpec(memory_space=pltpu.VMEM)
    return pl.pallas_call(
        functools.partial(_block_kernel, transpose),
        out_shape=jax.ShapeDtypeStruct((out_blocks * edge, x.shape[1]), jnp.float32),
        in_specs=[smem, smem, smem, vmem, vmem],
        out_specs=vmem,
    )(count.reshape(1), out_idx, in_idx, values, x)


def reduce_over(partial, axis, parts):
    rows = partial.shape[0] // parts
    pieces = partial.reshape(parts, rows, *partial.shape[1:])
    return lax.all_to_all(pieces, axis, 0, 0, tiled=True).sum(0)


def shards(block_values, block_rows, block_cols, block_counts, right_side, ridge, n_comp, n_feat):
    values = block_values[0, 0]
    slot_rows = block_rows[0, 0]
    slot_cols = block_cols[0, 0]
    count_of_slots = block_counts[0, 0]
    responses = right_side.shape[1]
    block_edge = values.shape[1]
    feat_rows = CB_DEV * block_edge
    own_rows = feat_rows // n_comp
    comp_index = lax.axis_index("comp")

    def backward(low_slab):
        return block_apply(values, count_of_slots, slot_cols, slot_rows, low_slab, CB_DEV, True)

    def forward(direction, extra=None):
        low = direction.astype(jnp.bfloat16)
        summed = block_apply(values, count_of_slots, slot_rows, slot_cols, low, RB_DEV, False)
        if extra is None:
            return reduce_over(summed, "feat", n_feat)
        pieces = summed.reshape(n_feat, -1, summed.shape[1])
        spread = jnp.broadcast_to(extra[None], (n_feat,) + extra.shape)
        landed = lax.all_to_all(
            jnp.concatenate([pieces, spread], axis=1), "feat", 0, 0, tiled=True
        ).sum(0)
        return landed[: pieces.shape[1]], landed[pieces.shape[1] :]

    core = comp_index % 2
    chip = comp_index // 2
    n_chips = n_comp // 2
    half_rows = feat_rows // 2
    siblings = [(i, i ^ 1) for i in range(n_comp)]
    same_core = [[i for i in range(n_comp) if i % 2 == p] for p in range(2)]

    def swap_with_sibling(x):
        return lax.ppermute(x, "comp", siblings)

    def reduce_gradient(partial):
        kept = lax.dynamic_slice_in_dim(partial, core * half_rows, half_rows, axis=0)
        sent = lax.dynamic_slice_in_dim(partial, (1 - core) * half_rows, half_rows, axis=0)
        chip_sum = kept + swap_with_sibling(sent)
        pieces = chip_sum.reshape(n_chips, own_rows, chip_sum.shape[1])
        landed = lax.all_to_all(pieces, "comp", 0, 0, tiled=True, axis_index_groups=same_core)
        return landed.sum(0)

    def gather_gradient(own):
        got = lax.all_gather(own, "comp", axis=0, tiled=False)
        by_chip = got[:, :own_rows].reshape(n_chips, 2, own_rows, own.shape[1])
        rows = by_chip.transpose(1, 0, 2, 3).reshape(feat_rows, own.shape[1])
        return rows, jnp.sum(got[:, own_rows:], axis=0)

    def own_part(full):
        return lax.dynamic_slice_in_dim(full, core * half_rows + chip * own_rows, own_rows, axis=0)

    def col_sq(x):
        return jnp.sum(x * x, axis=0)

    feat_index = lax.axis_index("feat")

    def gather_feat(own):
        spread = jnp.broadcast_to(own[None], (n_feat,) + own.shape)
        return lax.all_to_all(spread, "feat", 0, 0, tiled=True)

    def comp_total(stacked):
        spread = jnp.broadcast_to(stacked[None], (n_comp,) + stacked.shape)
        return lax.all_to_all(spread, "comp", 0, 0, tiled=True).sum(0)

    own_block = right_side.shape[0]
    residual_slab = gather_feat(right_side).reshape(RB_DEV * own_block, responses)

    def low_slab(slab):
        return slab.astype(jnp.bfloat16)

    gradient_own = reduce_gradient(backward(low_slab(residual_slab)))
    energy_own = col_sq(gradient_own)
    direction, _ = gather_gradient(gradient_own)
    energy = None
    solution = None
    for step_index in range(ITERS):
        last = step_index + 1 == ITERS
        if step_index > 0:
            gradient_own = reduce_gradient(backward(low_slab(residual_slab))) - ridge * own_part(
                solution
            )
            gradient, comp_energy = gather_gradient(
                jnp.concatenate([gradient_own, col_sq(gradient_own)[None]], axis=0)
            )
            gradient_image, next_energy = forward(gradient, comp_energy)
            next_energy = next_energy[0]
            conjugate = next_energy / energy
            direction = gradient + conjugate * direction
            image_rows = gradient_image + conjugate * image_rows
            energy = next_energy
        else:
            image_rows = forward(direction)
        if last:
            sums = [col_sq(image_rows), col_sq(own_part(direction))]
            if energy is None:
                sums.append(energy_own)
            spread = jnp.broadcast_to(jnp.stack(sums)[None], (n_feat, len(sums), responses))
            totals = comp_total(lax.all_to_all(spread, "feat", 0, 0, tiled=True).sum(0))
            if energy is None:
                energy = totals[2]
            image_energy, direction_energy = totals[0], totals[1]
        else:
            parts = [image_rows, col_sq(own_part(direction))[None]]
            if energy is None:
                parts.append(energy_own[None])
            gathered = gather_feat(jnp.concatenate(parts, axis=0))
            image_slab = gathered[:, :own_block].reshape(RB_DEV * own_block, responses)
            feat_sums = jnp.sum(gathered[:, own_block:], axis=0)
            totals = comp_total(jnp.concatenate([col_sq(image_slab)[None], feat_sums], axis=0))
            if energy is None:
                energy = totals[2]
            image_energy, direction_energy = totals[0], totals[1]
        step_size = energy / (image_energy + ridge * direction_energy)
        solution = step_size * direction if solution is None else solution + step_size * direction
        if last:
            own_residual = lax.dynamic_slice_in_dim(residual_slab, feat_index * own_block, own_block)
            residual = own_residual - step_size * image_rows
        else:
            residual_slab = residual_slab - step_size * image_slab
            image_rows = lax.dynamic_slice_in_dim(image_slab, feat_index * own_block, own_block)
    return (solution, residual)


def solution(mesh):
    placed = (
        P("comp", "feat", None, None, None),
        P("comp", "feat", None),
        P("comp", "feat", None),
        P("comp", "feat"),
        P(("comp", "feat"), None),
        P(),
    )
    n_comp = mesh.shape["comp"]
    n_feat = mesh.shape["feat"]

    def body(*args):
        return shards(*args, n_comp=n_comp, n_feat=n_feat)

    return jax.shard_map(
        body,
        mesh=mesh,
        in_specs=placed,
        out_specs=(P("feat", None), P(("comp", "feat"), None)),
        check_vma=False,
    )
```

```python
import functools

import jax
import jax.numpy as jnp
from jax import lax
from jax.experimental import pallas as pl
from jax.experimental.pallas import tpu as pltpu
from jax.sharding import PartitionSpec as P

RB_DEV = 16
CB_DEV = 14
ITERS = 2


def _block_kernel(transpose, pitch, count_ref, out_idx_ref, in_idx_ref, values_ref, x_ref, *rest):
    edge = values_ref.shape[1]
    out_ref = rest[-1]
    out_ref[...] = jnp.zeros_like(out_ref)
    if len(rest) == 2:
        extra_ref = rest[0]
        for b in range(out_ref.shape[0] // pitch):
            out_ref[pl.ds(b * pitch + edge, pitch - edge), :] = extra_ref[...]

    def body(s, carry):
        @pl.when(s < count_ref[0])
        def _():
            src = pl.multiple_of(in_idx_ref[s] * edge, edge)
            dst = pl.multiple_of(out_idx_ref[s] * pitch, 8)
            block = values_ref[s]
            x = x_ref[pl.ds(src, edge), :]
            if transpose:
                prod = lax.dot_general(
                    block, x, (((0,), (0,)), ((), ())), preferred_element_type=jnp.float32
                )
            else:
                prod = jnp.dot(block, x, preferred_element_type=jnp.float32)
            out_ref[pl.ds(dst, edge), :] += prod

        return carry

    lax.fori_loop(0, values_ref.shape[0], body, 0, unroll=True)


def block_apply(values, count, out_idx, in_idx, x, out_blocks, transpose, extra=None):
    edge = values.shape[1]
    pitch = edge if extra is None else edge + extra.shape[0]
    smem = pl.BlockSpec(memory_space=pltpu.SMEM)
    vmem = pl.BlockSpec(memory_space=pltpu.VMEM)
    operands = [count.reshape(1), out_idx, in_idx, values, x]
    if extra is not None:
        operands.append(extra)
    return pl.pallas_call(
        functools.partial(_block_kernel, transpose, pitch),
        out_shape=jax.ShapeDtypeStruct((out_blocks * pitch, x.shape[1]), jnp.float32),
        in_specs=[smem, smem, smem] + [vmem] * (len(operands) - 3),
        out_specs=vmem,
    )(*operands)


def reduce_over(partial, axis, parts):
    rows = partial.shape[0] // parts
    pieces = partial.reshape(parts, rows, *partial.shape[1:])
    return lax.all_to_all(pieces, axis, 0, 0, tiled=True).sum(0)


def shards(block_values, block_rows, block_cols, block_counts, right_side, ridge, n_comp, n_feat):
    values = block_values[0, 0]
    slot_rows = block_rows[0, 0]
    slot_cols = block_cols[0, 0]
    count_of_slots = block_counts[0, 0]
    responses = right_side.shape[1]
    block_edge = values.shape[1]
    feat_rows = CB_DEV * block_edge
    own_rows = feat_rows // n_comp
    comp_index = lax.axis_index("comp")

    def backward(low_slab):
        return block_apply(values, count_of_slots, slot_cols, slot_rows, low_slab, CB_DEV, True)

    def forward(direction, extra=None):
        low = direction.astype(jnp.bfloat16)
        if extra is None:
            summed = block_apply(values, count_of_slots, slot_rows, slot_cols, low, RB_DEV, False)
            return reduce_over(summed, "feat", n_feat)
        padded = jnp.zeros((8, extra.shape[1]), extra.dtype).at[: extra.shape[0]].set(extra)
        summed = block_apply(
            values, count_of_slots, slot_rows, slot_cols, low, RB_DEV, False, extra=padded
        )
        landed = reduce_over(summed, "feat", n_feat)
        return landed[:block_edge], landed[block_edge : block_edge + extra.shape[0]]

    core = comp_index % 2
    chip = comp_index // 2
    n_chips = n_comp // 2
    half_rows = feat_rows // 2
    siblings = [(i, i ^ 1) for i in range(n_comp)]
    same_core = [[i for i in range(n_comp) if i % 2 == p] for p in range(2)]

    def swap_with_sibling(x):
        return lax.ppermute(x, "comp", siblings)

    def reduce_gradient(partial):
        kept = lax.dynamic_slice_in_dim(partial, core * half_rows, half_rows, axis=0)
        sent = lax.dynamic_slice_in_dim(partial, (1 - core) * half_rows, half_rows, axis=0)
        chip_sum = kept + swap_with_sibling(sent)
        pieces = chip_sum.reshape(n_chips, own_rows, chip_sum.shape[1])
        landed = lax.all_to_all(pieces, "comp", 0, 0, tiled=True, axis_index_groups=same_core)
        return landed.sum(0)

    def gather_gradient(own):
        got = lax.all_gather(own, "comp", axis=0, tiled=False)
        by_chip = got[:, :own_rows].reshape(n_chips, 2, own_rows, own.shape[1])
        rows = by_chip.transpose(1, 0, 2, 3).reshape(feat_rows, own.shape[1])
        return rows, jnp.sum(got[:, own_rows:], axis=0)

    def own_part(full):
        return lax.dynamic_slice_in_dim(full, core * half_rows + chip * own_rows, own_rows, axis=0)

    def col_sq(x):
        return jnp.sum(x * x, axis=0)

    feat_index = lax.axis_index("feat")

    def gather_feat(own):
        spread = jnp.broadcast_to(own[None], (n_feat,) + own.shape)
        return lax.all_to_all(spread, "feat", 0, 0, tiled=True)

    def comp_total(stacked):
        spread = jnp.broadcast_to(stacked[None], (n_comp,) + stacked.shape)
        return lax.all_to_all(spread, "comp", 0, 0, tiled=True).sum(0)

    own_block = right_side.shape[0]
    residual_slab = gather_feat(right_side).reshape(RB_DEV * own_block, responses)

    def low_slab(slab):
        return slab.astype(jnp.bfloat16)

    gradient_own = reduce_gradient(backward(low_slab(residual_slab)))
    energy_own = col_sq(gradient_own)
    direction, _ = gather_gradient(gradient_own)
    energy = None
    solution = None
    for step_index in range(ITERS):
        last = step_index + 1 == ITERS
        if step_index > 0:
            gradient_own = reduce_gradient(backward(low_slab(residual_slab))) - ridge * own_part(
                solution
            )
            gradient, comp_energy = gather_gradient(
                jnp.concatenate([gradient_own, col_sq(gradient_own)[None]], axis=0)
            )
            gradient_image, next_energy = forward(gradient, comp_energy)
            next_energy = next_energy[0]
            conjugate = next_energy / energy
            direction = gradient + conjugate * direction
            image_rows = gradient_image + conjugate * image_rows
            energy = next_energy
        else:
            image_rows = forward(direction)
        if last:
            sums = [col_sq(image_rows), col_sq(own_part(direction))]
            if energy is None:
                sums.append(energy_own)
            spread = jnp.broadcast_to(jnp.stack(sums)[None], (n_feat, len(sums), responses))
            totals = comp_total(lax.all_to_all(spread, "feat", 0, 0, tiled=True).sum(0))
            if energy is None:
                energy = totals[2]
            image_energy, direction_energy = totals[0], totals[1]
        else:
            parts = [image_rows, col_sq(own_part(direction))[None]]
            if energy is None:
                parts.append(energy_own[None])
            gathered = gather_feat(jnp.concatenate(parts, axis=0))
            image_slab = gathered[:, :own_block].reshape(RB_DEV * own_block, responses)
            feat_sums = jnp.sum(gathered[:, own_block:], axis=0)
            totals = comp_total(jnp.concatenate([col_sq(image_slab)[None], feat_sums], axis=0))
            if energy is None:
                energy = totals[2]
            image_energy, direction_energy = totals[0], totals[1]
        step_size = energy / (image_energy + ridge * direction_energy)
        solution = step_size * direction if solution is None else solution + step_size * direction
        if last:
            own_residual = lax.dynamic_slice_in_dim(residual_slab, feat_index * own_block, own_block)
            residual = own_residual - step_size * image_rows
        else:
            residual_slab = residual_slab - step_size * image_slab
            image_rows = lax.dynamic_slice_in_dim(image_slab, feat_index * own_block, own_block)
    return (solution, residual)


def solution(mesh):
    placed = (
        P("comp", "feat", None, None, None),
        P("comp", "feat", None),
        P("comp", "feat", None),
        P("comp", "feat"),
        P(("comp", "feat"), None),
        P(),
    )
    n_comp = mesh.shape["comp"]
    n_feat = mesh.shape["feat"]

    def body(*args):
        return shards(*args, n_comp=n_comp, n_feat=n_feat)

    return jax.shard_map(
        body,
        mesh=mesh,
        in_specs=placed,
        out_specs=(P("feat", None), P(("comp", "feat"), None)),
        check_vma=False,
    )
```

```python
import functools

import jax
import jax.numpy as jnp
from jax import lax
from jax.experimental import pallas as pl
from jax.experimental.pallas import tpu as pltpu
from jax.sharding import PartitionSpec as P

RB_DEV = 16
CB_DEV = 14
ITERS = 2


def _block_kernel(transpose, pitch, count_ref, out_idx_ref, in_idx_ref, values_ref, x_ref, *rest):
    edge = values_ref.shape[1]
    out_ref = rest[-1]
    out_ref[...] = jnp.zeros_like(out_ref)
    if len(rest) == 2:
        extra_ref = rest[0]
        for b in range(out_ref.shape[0] // pitch):
            out_ref[pl.ds(b * pitch + edge, pitch - edge), :] = extra_ref[...]

    def body(s, carry):
        @pl.when(s < count_ref[0])
        def _():
            src = pl.multiple_of(in_idx_ref[s] * edge, edge)
            dst = pl.multiple_of(out_idx_ref[s] * pitch, 8)
            block = values_ref[s]
            x = x_ref[pl.ds(src, edge), :]
            if transpose:
                prod = lax.dot_general(
                    block, x, (((0,), (0,)), ((), ())), preferred_element_type=jnp.float32
                )
            else:
                prod = jnp.dot(block, x, preferred_element_type=jnp.float32)
            out_ref[pl.ds(dst, edge), :] += prod

        return carry

    lax.fori_loop(0, values_ref.shape[0], body, 0, unroll=True)


def block_apply(values, count, out_idx, in_idx, x, out_blocks, transpose, extra=None):
    edge = values.shape[1]
    pitch = edge if extra is None else edge + extra.shape[0]
    smem = pl.BlockSpec(memory_space=pltpu.SMEM)
    vmem = pl.BlockSpec(memory_space=pltpu.VMEM)
    operands = [count.reshape(1), out_idx, in_idx, values, x]
    if extra is not None:
        operands.append(extra)
    return pl.pallas_call(
        functools.partial(_block_kernel, transpose, pitch),
        out_shape=jax.ShapeDtypeStruct((out_blocks * pitch, x.shape[1]), jnp.float32),
        in_specs=[smem, smem, smem] + [vmem] * (len(operands) - 3),
        out_specs=vmem,
    )(*operands)


def reduce_over(partial, axis, parts):
    rows = partial.shape[0] // parts
    pieces = partial.reshape(parts, rows, *partial.shape[1:])
    return lax.all_to_all(pieces, axis, 0, 0, tiled=True).sum(0)


def shards(block_values, block_rows, block_cols, block_counts, right_side, ridge, n_comp, n_feat):
    values = block_values[0, 0]
    slot_rows = block_rows[0, 0]
    slot_cols = block_cols[0, 0]
    count_of_slots = block_counts[0, 0]
    responses = right_side.shape[1]
    block_edge = values.shape[1]
    feat_rows = CB_DEV * block_edge
    own_rows = feat_rows // n_comp
    comp_index = lax.axis_index("comp")

    def backward(low_slab):
        return block_apply(values, count_of_slots, slot_cols, slot_rows, low_slab, CB_DEV, True)

    def forward(direction, extra=None):
        low = direction.astype(jnp.bfloat16)
        if extra is None:
            summed = block_apply(values, count_of_slots, slot_rows, slot_cols, low, RB_DEV, False)
            return reduce_over(summed, "feat", n_feat)
        padded = jnp.zeros((8, extra.shape[1]), extra.dtype).at[: extra.shape[0]].set(extra)
        summed = block_apply(
            values, count_of_slots, slot_rows, slot_cols, low, RB_DEV, False, extra=padded
        )
        landed = reduce_over(summed, "feat", n_feat)
        return landed[:block_edge], landed[block_edge : block_edge + extra.shape[0]]

    core = comp_index % 2
    chip = comp_index // 2
    half_rows = feat_rows // 2
    quarter_rows = half_rows // 2
    pair = chip % 2
    n_groups = n_comp // 4
    siblings = [(i, i ^ 1) for i in range(n_comp)]
    neighbours = [(i, i ^ 2) for i in range(n_comp)]
    same_slot = [[i for i in range(n_comp) if i % 4 == g] for g in range(4)]

    def add_halves(x, keep, exchange, rows):
        kept = lax.dynamic_slice_in_dim(x, keep * rows, rows, axis=0)
        sent = lax.dynamic_slice_in_dim(x, (1 - keep) * rows, rows, axis=0)
        return kept + lax.ppermute(sent, "comp", exchange)

    def reduce_gradient(partial):
        chip_sum = add_halves(partial, core, siblings, half_rows)
        pair_sum = add_halves(chip_sum, pair, neighbours, quarter_rows)
        pieces = pair_sum.reshape(n_groups, own_rows, pair_sum.shape[1])
        landed = lax.all_to_all(pieces, "comp", 0, 0, tiled=True, axis_index_groups=same_slot)
        return landed.sum(0)

    def gather_gradient(own):
        got = lax.all_gather(own, "comp", axis=0, tiled=False)
        by_slot = got[:, :own_rows].reshape(n_groups, 2, 2, own_rows, own.shape[1])
        rows = by_slot.transpose(2, 1, 0, 3, 4).reshape(feat_rows, own.shape[1])
        return rows, jnp.sum(got[:, own_rows:], axis=0)

    def own_part(full):
        start = core * half_rows + pair * quarter_rows + (chip // 2) * own_rows
        return lax.dynamic_slice_in_dim(full, start, own_rows, axis=0)

    def col_sq(x):
        return jnp.sum(x * x, axis=0)

    feat_index = lax.axis_index("feat")

    def gather_feat(own):
        spread = jnp.broadcast_to(own[None], (n_feat,) + own.shape)
        return lax.all_to_all(spread, "feat", 0, 0, tiled=True)

    def comp_total(stacked):
        spread = jnp.broadcast_to(stacked[None], (n_comp,) + stacked.shape)
        return lax.all_to_all(spread, "comp", 0, 0, tiled=True).sum(0)

    own_block = right_side.shape[0]
    residual_slab = gather_feat(right_side).reshape(RB_DEV * own_block, responses)

    def low_slab(slab):
        return slab.astype(jnp.bfloat16)

    gradient_own = reduce_gradient(backward(low_slab(residual_slab)))
    energy_own = col_sq(gradient_own)
    direction, _ = gather_gradient(gradient_own)
    energy = None
    solution = None
    for step_index in range(ITERS):
        last = step_index + 1 == ITERS
        if step_index > 0:
            gradient_own = reduce_gradient(backward(low_slab(residual_slab))) - ridge * own_part(
                solution
            )
            gradient, comp_energy = gather_gradient(
                jnp.concatenate([gradient_own, col_sq(gradient_own)[None]], axis=0)
            )
            gradient_image, next_energy = forward(gradient, comp_energy)
            next_energy = next_energy[0]
            conjugate = next_energy / energy
            direction = gradient + conjugate * direction
            image_rows = gradient_image + conjugate * image_rows
            energy = next_energy
        else:
            image_rows = forward(direction)
        if last:
            sums = [col_sq(image_rows), col_sq(own_part(direction))]
            if energy is None:
                sums.append(energy_own)
            spread = jnp.broadcast_to(jnp.stack(sums)[None], (n_feat, len(sums), responses))
            totals = comp_total(lax.all_to_all(spread, "feat", 0, 0, tiled=True).sum(0))
            if energy is None:
                energy = totals[2]
            image_energy, direction_energy = totals[0], totals[1]
        else:
            parts = [image_rows, col_sq(own_part(direction))[None]]
            if energy is None:
                parts.append(energy_own[None])
            gathered = gather_feat(jnp.concatenate(parts, axis=0))
            image_slab = gathered[:, :own_block].reshape(RB_DEV * own_block, responses)
            feat_sums = jnp.sum(gathered[:, own_block:], axis=0)
            totals = comp_total(jnp.concatenate([col_sq(image_slab)[None], feat_sums], axis=0))
            if energy is None:
                energy = totals[2]
            image_energy, direction_energy = totals[0], totals[1]
        step_size = energy / (image_energy + ridge * direction_energy)
        solution = step_size * direction if solution is None else solution + step_size * direction
        if last:
            own_residual = lax.dynamic_slice_in_dim(residual_slab, feat_index * own_block, own_block)
            residual = own_residual - step_size * image_rows
        else:
            residual_slab = residual_slab - step_size * image_slab
            image_rows = lax.dynamic_slice_in_dim(image_slab, feat_index * own_block, own_block)
    return (solution, residual)


def solution(mesh):
    placed = (
        P("comp", "feat", None, None, None),
        P("comp", "feat", None),
        P("comp", "feat", None),
        P("comp", "feat"),
        P(("comp", "feat"), None),
        P(),
    )
    n_comp = mesh.shape["comp"]
    n_feat = mesh.shape["feat"]

    def body(*args):
        return shards(*args, n_comp=n_comp, n_feat=n_feat)

    return jax.shard_map(
        body,
        mesh=mesh,
        in_specs=placed,
        out_specs=(P("feat", None), P(("comp", "feat"), None)),
        check_vma=False,
    )
```

```python
import functools

import jax
import jax.numpy as jnp
from jax import lax
from jax.experimental import pallas as pl
from jax.experimental.pallas import tpu as pltpu
from jax.sharding import PartitionSpec as P

RB_DEV = 16
CB_DEV = 14
ITERS = 2


def _block_kernel(transpose, pitch, count_ref, out_idx_ref, in_idx_ref, values_ref, x_ref, *rest):
    edge = values_ref.shape[1]
    out_ref = rest[-1]
    out_ref[...] = jnp.zeros_like(out_ref)
    if len(rest) == 2:
        extra_ref = rest[0]
        for b in range(out_ref.shape[0] // pitch):
            out_ref[pl.ds(b * pitch + edge, pitch - edge), :] = extra_ref[...]

    def body(s, carry):
        @pl.when(s < count_ref[0])
        def _():
            src = pl.multiple_of(in_idx_ref[s] * edge, edge)
            dst = pl.multiple_of(out_idx_ref[s] * pitch, 8)
            block = values_ref[s]
            x = x_ref[pl.ds(src, edge), :].astype(values_ref.dtype)
            if transpose:
                prod = lax.dot_general(
                    block, x, (((0,), (0,)), ((), ())), preferred_element_type=jnp.float32
                )
            else:
                prod = jnp.dot(block, x, preferred_element_type=jnp.float32)
            out_ref[pl.ds(dst, edge), :] += prod

        return carry

    lax.fori_loop(0, values_ref.shape[0], body, 0, unroll=True)


def block_apply(values, count, out_idx, in_idx, x, out_blocks, transpose, extra=None):
    edge = values.shape[1]
    pitch = edge if extra is None else edge + extra.shape[0]
    smem = pl.BlockSpec(memory_space=pltpu.SMEM)
    vmem = pl.BlockSpec(memory_space=pltpu.VMEM)
    operands = [count.reshape(1), out_idx, in_idx, values, x]
    if extra is not None:
        operands.append(extra)
    return pl.pallas_call(
        functools.partial(_block_kernel, transpose, pitch),
        out_shape=jax.ShapeDtypeStruct((out_blocks * pitch, x.shape[1]), jnp.float32),
        in_specs=[smem, smem, smem] + [vmem] * (len(operands) - 3),
        out_specs=vmem,
    )(*operands)


def reduce_over(partial, axis, parts):
    rows = partial.shape[0] // parts
    pieces = partial.reshape(parts, rows, *partial.shape[1:])
    return lax.all_to_all(pieces, axis, 0, 0, tiled=True).sum(0)


def shards(block_values, block_rows, block_cols, block_counts, right_side, ridge, n_comp, n_feat):
    values = block_values[0, 0]
    slot_rows = block_rows[0, 0]
    slot_cols = block_cols[0, 0]
    count_of_slots = block_counts[0, 0]
    responses = right_side.shape[1]
    block_edge = values.shape[1]
    feat_rows = CB_DEV * block_edge
    own_rows = feat_rows // n_comp
    comp_index = lax.axis_index("comp")

    def backward(low_slab):
        return block_apply(values, count_of_slots, slot_cols, slot_rows, low_slab, CB_DEV, True)

    def forward(direction, extra=None):
        low = direction
        if extra is None:
            summed = block_apply(values, count_of_slots, slot_rows, slot_cols, low, RB_DEV, False)
            return reduce_over(summed, "feat", n_feat)
        padded = jnp.zeros((8, extra.shape[1]), extra.dtype).at[: extra.shape[0]].set(extra)
        summed = block_apply(
            values, count_of_slots, slot_rows, slot_cols, low, RB_DEV, False, extra=padded
        )
        landed = reduce_over(summed, "feat", n_feat)
        return landed[:block_edge], landed[block_edge : block_edge + extra.shape[0]]

    core = comp_index % 2
    chip = comp_index // 2
    half_rows = feat_rows // 2
    quarter_rows = half_rows // 2
    pair = chip % 2
    n_groups = n_comp // 4
    siblings = [(i, i ^ 1) for i in range(n_comp)]
    neighbours = [(i, i ^ 2) for i in range(n_comp)]
    same_slot = [[i for i in range(n_comp) if i % 4 == g] for g in range(4)]

    def add_halves(x, keep, exchange, rows):
        kept = lax.dynamic_slice_in_dim(x, keep * rows, rows, axis=0)
        sent = lax.dynamic_slice_in_dim(x, (1 - keep) * rows, rows, axis=0)
        return kept + lax.ppermute(sent, "comp", exchange)

    def reduce_gradient(partial):
        chip_sum = add_halves(partial, core, siblings, half_rows)
        pair_sum = add_halves(chip_sum, pair, neighbours, quarter_rows)
        pieces = pair_sum.reshape(n_groups, own_rows, pair_sum.shape[1])
        landed = lax.all_to_all(pieces, "comp", 0, 0, tiled=True, axis_index_groups=same_slot)
        return landed.sum(0)

    def gather_gradient(own):
        got = lax.all_gather(own, "comp", axis=0, tiled=False)
        by_slot = got[:, :own_rows].reshape(n_groups, 2, 2, own_rows, own.shape[1])
        rows = by_slot.transpose(2, 1, 0, 3, 4).reshape(feat_rows, own.shape[1])
        return rows, jnp.sum(got[:, own_rows:], axis=0)

    def own_part(full):
        start = core * half_rows + pair * quarter_rows + (chip // 2) * own_rows
        return lax.dynamic_slice_in_dim(full, start, own_rows, axis=0)

    def col_sq(x):
        return jnp.sum(x * x, axis=0)

    feat_index = lax.axis_index("feat")

    def gather_feat(own):
        spread = jnp.broadcast_to(own[None], (n_feat,) + own.shape)
        return lax.all_to_all(spread, "feat", 0, 0, tiled=True)

    def comp_total(stacked):
        spread = jnp.broadcast_to(stacked[None], (n_comp,) + stacked.shape)
        return lax.all_to_all(spread, "comp", 0, 0, tiled=True).sum(0)

    own_block = right_side.shape[0]
    residual_slab = gather_feat(right_side).reshape(RB_DEV * own_block, responses)

    def low_slab(slab):
        return slab

    gradient_own = reduce_gradient(backward(low_slab(residual_slab)))
    energy_own = col_sq(gradient_own)
    direction, _ = gather_gradient(gradient_own)
    energy = None
    solution = None
    for step_index in range(ITERS):
        last = step_index + 1 == ITERS
        if step_index > 0:
            gradient_own = reduce_gradient(backward(low_slab(residual_slab))) - ridge * own_part(
                solution
            )
            gradient, comp_energy = gather_gradient(
                jnp.concatenate([gradient_own, col_sq(gradient_own)[None]], axis=0)
            )
            gradient_image, next_energy = forward(gradient, comp_energy)
            next_energy = next_energy[0]
            conjugate = next_energy / energy
            direction = gradient + conjugate * direction
            image_rows = gradient_image + conjugate * image_rows
            energy = next_energy
        else:
            image_rows = forward(direction)
        if last:
            sums = [col_sq(image_rows), col_sq(own_part(direction))]
            if energy is None:
                sums.append(energy_own)
            spread = jnp.broadcast_to(jnp.stack(sums)[None], (n_feat, len(sums), responses))
            totals = comp_total(lax.all_to_all(spread, "feat", 0, 0, tiled=True).sum(0))
            if energy is None:
                energy = totals[2]
            image_energy, direction_energy = totals[0], totals[1]
        else:
            parts = [image_rows, col_sq(own_part(direction))[None]]
            if energy is None:
                parts.append(energy_own[None])
            gathered = gather_feat(jnp.concatenate(parts, axis=0))
            image_slab = gathered[:, :own_block].reshape(RB_DEV * own_block, responses)
            feat_sums = jnp.sum(gathered[:, own_block:], axis=0)
            totals = comp_total(jnp.concatenate([col_sq(image_slab)[None], feat_sums], axis=0))
            if energy is None:
                energy = totals[2]
            image_energy, direction_energy = totals[0], totals[1]
        step_size = energy / (image_energy + ridge * direction_energy)
        solution = step_size * direction if solution is None else solution + step_size * direction
        if last:
            own_residual = lax.dynamic_slice_in_dim(residual_slab, feat_index * own_block, own_block)
            residual = own_residual - step_size * image_rows
        else:
            residual_slab = residual_slab - step_size * image_slab
            image_rows = lax.dynamic_slice_in_dim(image_slab, feat_index * own_block, own_block)
    return (solution, residual)


def solution(mesh):
    placed = (
        P("comp", "feat", None, None, None),
        P("comp", "feat", None),
        P("comp", "feat", None),
        P("comp", "feat"),
        P(("comp", "feat"), None),
        P(),
    )
    n_comp = mesh.shape["comp"]
    n_feat = mesh.shape["feat"]

    def body(*args):
        return shards(*args, n_comp=n_comp, n_feat=n_feat)

    return jax.shard_map(
        body,
        mesh=mesh,
        in_specs=placed,
        out_specs=(P("feat", None), P(("comp", "feat"), None)),
        check_vma=False,
    )
```

```python
import functools

import jax
import jax.numpy as jnp
from jax import lax
from jax.experimental import pallas as pl
from jax.experimental.pallas import tpu as pltpu
from jax.sharding import PartitionSpec as P

RB_DEV = 16
CB_DEV = 14
ITERS = 2


def _block_kernel(transpose, pitch, count_ref, out_idx_ref, in_idx_ref, values_ref, x_ref, *rest):
    edge = values_ref.shape[1]
    out_ref = rest[-1]
    out_ref[...] = jnp.zeros_like(out_ref)
    if len(rest) == 2:
        extra_ref = rest[0]
        for b in range(out_ref.shape[0] // pitch):
            out_ref[pl.ds(b * pitch + edge, pitch - edge), :] = extra_ref[...]

    def body(s, carry):
        @pl.when(s < count_ref[0])
        def _():
            src = pl.multiple_of(in_idx_ref[s] * edge, edge)
            dst = pl.multiple_of(out_idx_ref[s] * pitch, 8)
            block = values_ref[s]
            x = x_ref[pl.ds(src, edge), :]
            if transpose:
                prod = lax.dot_general(
                    block, x, (((0,), (0,)), ((), ())), preferred_element_type=jnp.float32
                )
            else:
                prod = jnp.dot(block, x, preferred_element_type=jnp.float32)
            out_ref[pl.ds(dst, edge), :] += prod

        return carry

    lax.fori_loop(0, values_ref.shape[0], body, 0, unroll=True)


def block_apply(values, count, out_idx, in_idx, x, out_blocks, transpose, extra=None):
    edge = values.shape[1]
    pitch = edge if extra is None else edge + extra.shape[0]
    smem = pl.BlockSpec(memory_space=pltpu.SMEM)
    vmem = pl.BlockSpec(memory_space=pltpu.VMEM)
    operands = [count.reshape(1), out_idx, in_idx, values, x]
    if extra is not None:
        operands.append(extra)
    return pl.pallas_call(
        functools.partial(_block_kernel, transpose, pitch),
        out_shape=jax.ShapeDtypeStruct((out_blocks * pitch, x.shape[1]), jnp.float32),
        in_specs=[smem, smem, smem] + [vmem] * (len(operands) - 3),
        out_specs=vmem,
    )(*operands)


def _split_kernel(count_ref, out_idx_ref, in_idx_ref, core_ref, values_ref, x_ref, kept_ref, sent_ref):
    edge = values_ref.shape[1]
    half = kept_ref.shape[0] // edge
    kept_ref[...] = jnp.zeros_like(kept_ref)
    sent_ref[...] = jnp.zeros_like(sent_ref)

    def body(s, carry):
        @pl.when(s < count_ref[0])
        def _():
            src = pl.multiple_of(in_idx_ref[s] * edge, edge)
            block_index = out_idx_ref[s]
            dst = pl.multiple_of((block_index % half) * edge, edge)
            x = x_ref[pl.ds(src, edge), :].astype(values_ref.dtype)
            prod = jnp.dot(values_ref[s], x, preferred_element_type=jnp.float32)
            mine = block_index // half == core_ref[0]

            @pl.when(mine)
            def _():
                kept_ref[pl.ds(dst, edge), :] += prod

            @pl.when(jnp.logical_not(mine))
            def _():
                sent_ref[pl.ds(dst, edge), :] += prod

        return carry

    lax.fori_loop(0, values_ref.shape[0], body, 0)


def split_apply(values, count, out_idx, in_idx, x, core):
    edge = values.shape[1]
    rows = CB_DEV * edge // 2
    smem = pl.BlockSpec(memory_space=pltpu.SMEM)
    vmem = pl.BlockSpec(memory_space=pltpu.VMEM)
    half = jax.ShapeDtypeStruct((rows, x.shape[1]), jnp.float32)
    return pl.pallas_call(
        _split_kernel,
        out_shape=(half, half),
        in_specs=[smem, smem, smem, smem, vmem, vmem],
        out_specs=(vmem, vmem),
    )(count.reshape(1), out_idx, in_idx, core.astype(jnp.int32).reshape(1), values, x)


def reduce_over(partial, axis, parts):
    rows = partial.shape[0] // parts
    pieces = partial.reshape(parts, rows, *partial.shape[1:])
    return lax.all_to_all(pieces, axis, 0, 0, tiled=True).sum(0)


def shards(block_values, block_rows, block_cols, block_counts, right_side, ridge, n_comp, n_feat):
    values = block_values[0, 0]
    slot_rows = block_rows[0, 0]
    slot_cols = block_cols[0, 0]
    count_of_slots = block_counts[0, 0]
    responses = right_side.shape[1]
    block_edge = values.shape[1]
    feat_rows = CB_DEV * block_edge
    own_rows = feat_rows // n_comp
    comp_index = lax.axis_index("comp")
    core = comp_index % 2

    values_t = jnp.swapaxes(values, 1, 2)

    def backward(low_slab):
        return split_apply(values_t, count_of_slots, slot_cols, slot_rows, low_slab, core)

    def forward(direction, extra=None):
        low = direction.astype(jnp.bfloat16)
        if extra is None:
            summed = block_apply(values, count_of_slots, slot_rows, slot_cols, low, RB_DEV, False)
            return reduce_over(summed, "feat", n_feat)
        padded = jnp.zeros((8, extra.shape[1]), extra.dtype).at[: extra.shape[0]].set(extra)
        summed = block_apply(
            values, count_of_slots, slot_rows, slot_cols, low, RB_DEV, False, extra=padded
        )
        landed = reduce_over(summed, "feat", n_feat)
        return landed[:block_edge], landed[block_edge : block_edge + extra.shape[0]]

    chip = comp_index // 2
    n_chips = n_comp // 2
    half_rows = feat_rows // 2
    siblings = [(i, i ^ 1) for i in range(n_comp)]
    same_core = [[i for i in range(n_comp) if i % 2 == p] for p in range(2)]

    def swap_with_sibling(x):
        return lax.ppermute(x, "comp", siblings)

    def reduce_gradient(halves):
        kept, sent = halves
        chip_sum = kept + swap_with_sibling(sent)
        pieces = chip_sum.reshape(n_chips, own_rows, chip_sum.shape[1])
        landed = lax.all_to_all(pieces, "comp", 0, 0, tiled=True, axis_index_groups=same_core)
        return landed.sum(0)

    def gather_gradient(own):
        got = lax.all_gather(own, "comp", axis=0, tiled=False)
        by_chip = got[:, :own_rows].reshape(n_chips, 2, own_rows, own.shape[1])
        rows = by_chip.transpose(1, 0, 2, 3).reshape(feat_rows, own.shape[1])
        return rows, jnp.sum(got[:, own_rows:], axis=0)

    def own_part(full):
        return lax.dynamic_slice_in_dim(full, core * half_rows + chip * own_rows, own_rows, axis=0)

    def col_sq(x):
        return jnp.sum(x * x, axis=0)

    feat_index = lax.axis_index("feat")

    def gather_feat(own):
        spread = jnp.broadcast_to(own[None], (n_feat,) + own.shape)
        return lax.all_to_all(spread, "feat", 0, 0, tiled=True)

    def comp_total(stacked):
        spread = jnp.broadcast_to(stacked[None], (n_comp,) + stacked.shape)
        return lax.all_to_all(spread, "comp", 0, 0, tiled=True).sum(0)

    own_block = right_side.shape[0]
    residual_slab = gather_feat(right_side).reshape(RB_DEV * own_block, responses)

    def low_slab(slab):
        return slab.astype(jnp.bfloat16)

    gradient_own = reduce_gradient(backward(low_slab(residual_slab)))
    energy_own = col_sq(gradient_own)
    direction, _ = gather_gradient(gradient_own)
    energy = None
    solution = None
    for step_index in range(ITERS):
        last = step_index + 1 == ITERS
        if step_index > 0:
            gradient_own = reduce_gradient(backward(low_slab(residual_slab))) - ridge * own_part(
                solution
            )
            gradient, comp_energy = gather_gradient(
                jnp.concatenate([gradient_own, col_sq(gradient_own)[None]], axis=0)
            )
            gradient_image, next_energy = forward(gradient, comp_energy)
            next_energy = next_energy[0]
            conjugate = next_energy / energy
            direction = gradient + conjugate * direction
            image_rows = gradient_image + conjugate * image_rows
            energy = next_energy
        else:
            image_rows = forward(direction)
        if last:
            sums = [col_sq(image_rows), col_sq(own_part(direction))]
            if energy is None:
                sums.append(energy_own)
            spread = jnp.broadcast_to(jnp.stack(sums)[None], (n_feat, len(sums), responses))
            totals = comp_total(lax.all_to_all(spread, "feat", 0, 0, tiled=True).sum(0))
            if energy is None:
                energy = totals[2]
            image_energy, direction_energy = totals[0], totals[1]
        else:
            parts = [image_rows, col_sq(own_part(direction))[None]]
            if energy is None:
                parts.append(energy_own[None])
            gathered = gather_feat(jnp.concatenate(parts, axis=0))
            image_slab = gathered[:, :own_block].reshape(RB_DEV * own_block, responses)
            feat_sums = jnp.sum(gathered[:, own_block:], axis=0)
            totals = comp_total(jnp.concatenate([col_sq(image_slab)[None], feat_sums], axis=0))
            if energy is None:
                energy = totals[2]
            image_energy, direction_energy = totals[0], totals[1]
        step_size = energy / (image_energy + ridge * direction_energy)
        solution = step_size * direction if solution is None else solution + step_size * direction
        if last:
            own_residual = lax.dynamic_slice_in_dim(residual_slab, feat_index * own_block, own_block)
            residual = own_residual - step_size * image_rows
        else:
            residual_slab = residual_slab - step_size * image_slab
            image_rows = lax.dynamic_slice_in_dim(image_slab, feat_index * own_block, own_block)
    return (solution, residual)


def solution(mesh):
    placed = (
        P("comp", "feat", None, None, None),
        P("comp", "feat", None),
        P("comp", "feat", None),
        P("comp", "feat"),
        P(("comp", "feat"), None),
        P(),
    )
    n_comp = mesh.shape["comp"]
    n_feat = mesh.shape["feat"]

    def body(*args):
        return shards(*args, n_comp=n_comp, n_feat=n_feat)

    return jax.shard_map(
        body,
        mesh=mesh,
        in_specs=placed,
        out_specs=(P("feat", None), P(("comp", "feat"), None)),
        check_vma=False,
    )
```

```python
import functools

import jax
import jax.numpy as jnp
from jax import lax
from jax.experimental import pallas as pl
from jax.experimental.pallas import tpu as pltpu
from jax.sharding import PartitionSpec as P

RB_DEV = 16
CB_DEV = 14
ITERS = 2


def _block_kernel(transpose, pitch, count_ref, out_idx_ref, in_idx_ref, values_ref, x_ref, *rest):
    edge = values_ref.shape[1]
    out_ref = rest[-1]
    out_ref[...] = jnp.zeros_like(out_ref)
    if len(rest) == 2:
        extra_ref = rest[0]
        for b in range(out_ref.shape[0] // pitch):
            out_ref[pl.ds(b * pitch + edge, pitch - edge), :] = extra_ref[...]

    def body(s, carry):
        @pl.when(s < count_ref[0])
        def _():
            src = pl.multiple_of(in_idx_ref[s] * edge, edge)
            dst = pl.multiple_of(out_idx_ref[s] * pitch, 8)
            block = values_ref[s]
            x = x_ref[pl.ds(src, edge), :]
            if transpose:
                prod = lax.dot_general(
                    block, x, (((0,), (0,)), ((), ())), preferred_element_type=jnp.float32
                )
            else:
                prod = jnp.dot(block, x, preferred_element_type=jnp.float32)
            out_ref[pl.ds(dst, edge), :] += prod

        return carry

    lax.fori_loop(0, values_ref.shape[0], body, 0, unroll=True)


def block_apply(values, count, out_idx, in_idx, x, out_blocks, transpose, extra=None):
    edge = values.shape[1]
    pitch = edge if extra is None else edge + extra.shape[0]
    smem = pl.BlockSpec(memory_space=pltpu.SMEM)
    vmem = pl.BlockSpec(memory_space=pltpu.VMEM)
    operands = [count.reshape(1), out_idx, in_idx, values, x]
    if extra is not None:
        operands.append(extra)
    return pl.pallas_call(
        functools.partial(_block_kernel, transpose, pitch),
        out_shape=jax.ShapeDtypeStruct((out_blocks * pitch, x.shape[1]), jnp.float32),
        in_specs=[smem, smem, smem] + [vmem] * (len(operands) - 3),
        out_specs=vmem,
    )(*operands)


def reduce_over(partial, axis, parts):
    rows = partial.shape[0] // parts
    pieces = partial.reshape(parts, rows, *partial.shape[1:])
    return lax.all_to_all(pieces, axis, 0, 0, tiled=True).sum(0)


def shards(block_values, block_rows, block_cols, block_counts, right_side, ridge, n_comp, n_feat):
    values = block_values[0, 0]
    slot_rows = block_rows[0, 0]
    slot_cols = block_cols[0, 0]
    count_of_slots = block_counts[0, 0]
    responses = right_side.shape[1]
    block_edge = values.shape[1]
    feat_rows = CB_DEV * block_edge
    own_rows = feat_rows // n_comp
    comp_index = lax.axis_index("comp")

    def backward(low_slab):
        return block_apply(values, count_of_slots, slot_cols, slot_rows, low_slab, CB_DEV, True)

    def forward(direction, extra=None):
        low = direction.astype(jnp.bfloat16)
        if extra is None:
            summed = block_apply(values, count_of_slots, slot_rows, slot_cols, low, RB_DEV, False)
            return reduce_over(summed, "feat", n_feat)
        padded = jnp.zeros((8, extra.shape[1]), extra.dtype).at[: extra.shape[0]].set(extra)
        summed = block_apply(
            values, count_of_slots, slot_rows, slot_cols, low, RB_DEV, False, extra=padded
        )
        landed = reduce_over(summed, "feat", n_feat)
        return landed[:block_edge], landed[block_edge : block_edge + extra.shape[0]]

    core = comp_index % 2
    chip = comp_index // 2
    n_chips = n_comp // 2
    half_rows = feat_rows // 2
    siblings = [(i, i ^ 1) for i in range(n_comp)]
    same_core = [[i for i in range(n_comp) if i % 2 == p] for p in range(2)]

    def swap_with_sibling(x):
        return lax.ppermute(x, "comp", siblings)

    def reduce_gradient(partial):
        kept = lax.dynamic_slice_in_dim(partial, core * half_rows, half_rows, axis=0)
        sent = lax.dynamic_slice_in_dim(partial, (1 - core) * half_rows, half_rows, axis=0)
        chip_sum = kept + swap_with_sibling(sent)
        pieces = chip_sum.reshape(n_chips, own_rows, chip_sum.shape[1])
        landed = lax.all_to_all(pieces, "comp", 0, 0, tiled=True, axis_index_groups=same_core)
        return landed.sum(0)

    def gather_gradient(own):
        got = lax.all_gather(own, "comp", axis=0, tiled=False)
        by_chip = got[:, :own_rows].reshape(n_chips, 2, own_rows, own.shape[1])
        rows = by_chip.transpose(1, 0, 2, 3).reshape(feat_rows, own.shape[1])
        return rows, jnp.sum(got[:, own_rows:], axis=0)

    def own_part(full):
        return lax.dynamic_slice_in_dim(full, core * half_rows + chip * own_rows, own_rows, axis=0)

    def col_sq(x):
        return jnp.sum(x * x, axis=0)

    feat_index = lax.axis_index("feat")

    def gather_feat(own):
        spread = jnp.broadcast_to(own[None], (n_feat,) + own.shape)
        return lax.all_to_all(spread, "feat", 0, 0, tiled=True)

    def comp_total(stacked):
        spread = jnp.broadcast_to(stacked[None], (n_comp,) + stacked.shape)
        return lax.all_to_all(spread, "comp", 0, 0, tiled=True).sum(0)

    own_block = right_side.shape[0]
    residual_slab = gather_feat(right_side).reshape(RB_DEV * own_block, responses)

    def low_slab(slab):
        return slab.astype(jnp.bfloat16)

    zero_solution = 0.0 * residual_slab[:feat_rows]
    gradient_own = reduce_gradient(backward(low_slab(residual_slab))) - ridge * own_part(zero_solution)
    energy_own = col_sq(gradient_own)
    direction, _ = gather_gradient(gradient_own)
    energy = None
    solution = None
    for step_index in range(ITERS):
        last = step_index + 1 == ITERS
        if step_index > 0:
            gradient_own = reduce_gradient(backward(low_slab(residual_slab))) - ridge * own_part(
                solution
            )
            gradient, comp_energy = gather_gradient(
                jnp.concatenate([gradient_own, col_sq(gradient_own)[None]], axis=0)
            )
            gradient_image, next_energy = forward(gradient, comp_energy)
            next_energy = next_energy[0]
            conjugate = next_energy / energy
            direction = gradient + conjugate * direction
            image_rows = gradient_image + conjugate * image_rows
            energy = next_energy
        else:
            image_rows = forward(direction)
        if last:
            sums = [col_sq(image_rows), col_sq(own_part(direction))]
            if energy is None:
                sums.append(energy_own)
            spread = jnp.broadcast_to(jnp.stack(sums)[None], (n_feat, len(sums), responses))
            totals = comp_total(lax.all_to_all(spread, "feat", 0, 0, tiled=True).sum(0))
            if energy is None:
                energy = totals[2]
            image_energy, direction_energy = totals[0], totals[1]
        else:
            parts = [image_rows, col_sq(own_part(direction))[None]]
            if energy is None:
                parts.append(energy_own[None])
            gathered = gather_feat(jnp.concatenate(parts, axis=0))
            image_slab = gathered[:, :own_block].reshape(RB_DEV * own_block, responses)
            feat_sums = jnp.sum(gathered[:, own_block:], axis=0)
            totals = comp_total(jnp.concatenate([col_sq(image_slab)[None], feat_sums], axis=0))
            if energy is None:
                energy = totals[2]
            image_energy, direction_energy = totals[0], totals[1]
        step_size = energy / (image_energy + ridge * direction_energy)
        solution = step_size * direction if solution is None else solution + step_size * direction
        if last:
            own_residual = lax.dynamic_slice_in_dim(residual_slab, feat_index * own_block, own_block)
            residual = own_residual - step_size * image_rows
        else:
            residual_slab = residual_slab - step_size * image_slab
            image_rows = lax.dynamic_slice_in_dim(image_slab, feat_index * own_block, own_block)
    return (solution, residual)


def solution(mesh):
    placed = (
        P("comp", "feat", None, None, None),
        P("comp", "feat", None),
        P("comp", "feat", None),
        P("comp", "feat"),
        P(("comp", "feat"), None),
        P(),
    )
    n_comp = mesh.shape["comp"]
    n_feat = mesh.shape["feat"]

    def body(*args):
        return shards(*args, n_comp=n_comp, n_feat=n_feat)

    return jax.shard_map(
        body,
        mesh=mesh,
        in_specs=placed,
        out_specs=(P("feat", None), P(("comp", "feat"), None)),
        check_vma=False,
    )
```

```python
import functools

import jax
import jax.numpy as jnp
from jax import lax
from jax.experimental import pallas as pl
from jax.experimental.pallas import tpu as pltpu
from jax.sharding import PartitionSpec as P

RB_DEV = 16
CB_DEV = 14
ITERS = 2


def _block_kernel(transpose, pitch, count_ref, out_idx_ref, in_idx_ref, values_ref, x_ref, *rest):
    edge = values_ref.shape[1]
    out_ref = rest[-1]
    out_ref[...] = jnp.zeros_like(out_ref)
    if len(rest) == 2:
        extra_ref = rest[0]
        for b in range(out_ref.shape[0] // pitch):
            out_ref[pl.ds(b * pitch + edge, pitch - edge), :] = extra_ref[...]

    def body(s, carry):
        @pl.when(s < count_ref[0])
        def _():
            src = pl.multiple_of(in_idx_ref[s] * edge, edge)
            dst = pl.multiple_of(out_idx_ref[s] * pitch, 8)
            block = values_ref[s]
            x = x_ref[pl.ds(src, edge), :]
            if transpose:
                prod = lax.dot_general(
                    block, x, (((0,), (0,)), ((), ())), preferred_element_type=jnp.float32
                )
            else:
                prod = jnp.dot(block, x, preferred_element_type=jnp.float32)
            out_ref[pl.ds(dst, edge), :] += prod

        return carry

    lax.fori_loop(0, values_ref.shape[0], body, 0, unroll=True)


def block_apply(values, count, out_idx, in_idx, x, out_blocks, transpose, extra=None):
    edge = values.shape[1]
    pitch = edge if extra is None else edge + extra.shape[0]
    smem = pl.BlockSpec(memory_space=pltpu.SMEM)
    vmem = pl.BlockSpec(memory_space=pltpu.VMEM)
    operands = [count.reshape(1), out_idx, in_idx, values, x]
    if extra is not None:
        operands.append(extra)
    return pl.pallas_call(
        functools.partial(_block_kernel, transpose, pitch),
        out_shape=jax.ShapeDtypeStruct((out_blocks * pitch, x.shape[1]), jnp.float32),
        in_specs=[smem, smem, smem] + [vmem] * (len(operands) - 3),
        out_specs=vmem,
    )(*operands)


def reduce_over(partial, axis, parts):
    rows = partial.shape[0] // parts
    pieces = partial.reshape(parts, rows, *partial.shape[1:])
    return lax.all_to_all(pieces, axis, 0, 0, tiled=True).sum(0)


def shards(block_values, block_rows, block_cols, block_counts, right_side, ridge, n_comp, n_feat):
    values = block_values[0, 0]
    slot_rows = block_rows[0, 0]
    slot_cols = block_cols[0, 0]
    count_of_slots = block_counts[0, 0]
    responses = right_side.shape[1]
    block_edge = values.shape[1]
    feat_rows = CB_DEV * block_edge
    own_rows = feat_rows // n_comp
    comp_index = lax.axis_index("comp")

    def backward(low_slab):
        return block_apply(values, count_of_slots, slot_cols, slot_rows, low_slab, CB_DEV, True)

    def forward(direction, extra=None):
        low = direction.astype(jnp.bfloat16)
        if extra is None:
            summed = block_apply(values, count_of_slots, slot_rows, slot_cols, low, RB_DEV, False)
            return reduce_over(summed, "feat", n_feat)
        padded = jnp.zeros((8, extra.shape[1]), extra.dtype).at[: extra.shape[0]].set(extra)
        summed = block_apply(
            values, count_of_slots, slot_rows, slot_cols, low, RB_DEV, False, extra=padded
        )
        landed = reduce_over(summed, "feat", n_feat)
        return landed[:block_edge], landed[block_edge : block_edge + extra.shape[0]]

    core = comp_index % 2
    chip = comp_index // 2
    n_chips = n_comp // 2
    half_rows = feat_rows // 2
    siblings = [(i, i ^ 1) for i in range(n_comp)]
    same_core = [[i for i in range(n_comp) if i % 2 == p] for p in range(2)]

    def swap_with_sibling(x):
        return lax.ppermute(x, "comp", siblings)

    def reduce_gradient(partial):
        kept = lax.dynamic_slice_in_dim(partial, core * half_rows, half_rows, axis=0)
        sent = lax.dynamic_slice_in_dim(partial, (1 - core) * half_rows, half_rows, axis=0)
        chip_sum = kept + swap_with_sibling(sent)
        pieces = chip_sum.reshape(n_chips, own_rows, chip_sum.shape[1])
        landed = lax.all_to_all(pieces, "comp", 0, 0, tiled=True, axis_index_groups=same_core)
        return landed.sum(0)

    def gather_gradient(own):
        got = lax.all_gather(own, "comp", axis=0, tiled=False)
        by_chip = got[:, :own_rows].reshape(n_chips, 2, own_rows, own.shape[1])
        rows = by_chip.transpose(1, 0, 2, 3).reshape(feat_rows, own.shape[1])
        return rows, jnp.sum(got[:, own_rows:], axis=0)

    def own_part(full):
        return lax.dynamic_slice_in_dim(full, core * half_rows + chip * own_rows, own_rows, axis=0)

    def col_sq(x):
        return jnp.sum(x * x, axis=0)

    feat_index = lax.axis_index("feat")

    def gather_feat(own):
        spread = jnp.broadcast_to(own[None], (n_feat,) + own.shape)
        return lax.all_to_all(spread, "feat", 0, 0, tiled=True)

    def comp_total(stacked):
        total = stacked
        distance = 1
        while distance < n_comp:
            partner = [(i, i ^ distance) for i in range(n_comp)]
            total = total + lax.ppermute(total, "comp", partner)
            distance *= 2
        return total

    own_block = right_side.shape[0]
    residual_slab = gather_feat(right_side).reshape(RB_DEV * own_block, responses)

    def low_slab(slab):
        return slab.astype(jnp.bfloat16)

    gradient_own = reduce_gradient(backward(low_slab(residual_slab)))
    energy_own = col_sq(gradient_own)
    direction, _ = gather_gradient(gradient_own)
    energy = None
    solution = None
    for step_index in range(ITERS):
        last = step_index + 1 == ITERS
        if step_index > 0:
            gradient_own = reduce_gradient(backward(low_slab(residual_slab))) - ridge * own_part(
                solution
            )
            gradient, comp_energy = gather_gradient(
                jnp.concatenate([gradient_own, col_sq(gradient_own)[None]], axis=0)
            )
            gradient_image, next_energy = forward(gradient, comp_energy)
            next_energy = next_energy[0]
            conjugate = next_energy / energy
            direction = gradient + conjugate * direction
            image_rows = gradient_image + conjugate * image_rows
            energy = next_energy
        else:
            image_rows = forward(direction)
        if last:
            sums = [col_sq(image_rows), col_sq(own_part(direction))]
            if energy is None:
                sums.append(energy_own)
            spread = jnp.broadcast_to(jnp.stack(sums)[None], (n_feat, len(sums), responses))
            totals = comp_total(lax.all_to_all(spread, "feat", 0, 0, tiled=True).sum(0))
            if energy is None:
                energy = totals[2]
            image_energy, direction_energy = totals[0], totals[1]
        else:
            parts = [image_rows, col_sq(own_part(direction))[None]]
            if energy is None:
                parts.append(energy_own[None])
            gathered = gather_feat(jnp.concatenate(parts, axis=0))
            image_slab = gathered[:, :own_block].reshape(RB_DEV * own_block, responses)
            feat_sums = jnp.sum(gathered[:, own_block:], axis=0)
            totals = comp_total(jnp.concatenate([col_sq(image_slab)[None], feat_sums], axis=0))
            if energy is None:
                energy = totals[2]
            image_energy, direction_energy = totals[0], totals[1]
        step_size = energy / (image_energy + ridge * direction_energy)
        solution = step_size * direction if solution is None else solution + step_size * direction
        if last:
            own_residual = lax.dynamic_slice_in_dim(residual_slab, feat_index * own_block, own_block)
            residual = own_residual - step_size * image_rows
        else:
            residual_slab = residual_slab - step_size * image_slab
            image_rows = lax.dynamic_slice_in_dim(image_slab, feat_index * own_block, own_block)
    return (solution, residual)


def solution(mesh):
    placed = (
        P("comp", "feat", None, None, None),
        P("comp", "feat", None),
        P("comp", "feat", None),
        P("comp", "feat"),
        P(("comp", "feat"), None),
        P(),
    )
    n_comp = mesh.shape["comp"]
    n_feat = mesh.shape["feat"]

    def body(*args):
        return shards(*args, n_comp=n_comp, n_feat=n_feat)

    return jax.shard_map(
        body,
        mesh=mesh,
        in_specs=placed,
        out_specs=(P("feat", None), P(("comp", "feat"), None)),
        check_vma=False,
    )
```

```python
import functools

import jax
import jax.numpy as jnp
from jax import lax
from jax.experimental import pallas as pl
from jax.experimental.pallas import tpu as pltpu
from jax.sharding import PartitionSpec as P

RB_DEV = 16
CB_DEV = 14
ITERS = 2


def _block_kernel(transpose, pitch, count_ref, out_idx_ref, in_idx_ref, values_ref, x_ref, *rest):
    edge = values_ref.shape[1]
    out_ref = rest[-1]
    out_ref[...] = jnp.zeros_like(out_ref)
    if len(rest) == 2:
        extra_ref = rest[0]
        for b in range(out_ref.shape[0] // pitch):
            out_ref[pl.ds(b * pitch + edge, pitch - edge), :] = extra_ref[...]

    def body(s, carry):
        src = pl.multiple_of(in_idx_ref[s] * edge, edge)
        dst = pl.multiple_of(out_idx_ref[s] * pitch, 8)
        block = values_ref[s]
        x = x_ref[pl.ds(src, edge), :]
        if transpose:
            prod = lax.dot_general(
                block, x, (((0,), (0,)), ((), ())), preferred_element_type=jnp.float32
            )
        else:
            prod = jnp.dot(block, x, preferred_element_type=jnp.float32)
        live = s < count_ref[0]
        out_ref[pl.ds(dst, edge), :] += jnp.where(live, prod, 0.0)
        return carry

    lax.fori_loop(0, values_ref.shape[0], body, 0, unroll=True)


def block_apply(values, count, out_idx, in_idx, x, out_blocks, transpose, extra=None):
    edge = values.shape[1]
    pitch = edge if extra is None else edge + extra.shape[0]
    smem = pl.BlockSpec(memory_space=pltpu.SMEM)
    vmem = pl.BlockSpec(memory_space=pltpu.VMEM)
    operands = [count.reshape(1), out_idx, in_idx, values, x]
    if extra is not None:
        operands.append(extra)
    return pl.pallas_call(
        functools.partial(_block_kernel, transpose, pitch),
        out_shape=jax.ShapeDtypeStruct((out_blocks * pitch, x.shape[1]), jnp.float32),
        in_specs=[smem, smem, smem] + [vmem] * (len(operands) - 3),
        out_specs=vmem,
    )(*operands)


def reduce_over(partial, axis, parts):
    rows = partial.shape[0] // parts
    pieces = partial.reshape(parts, rows, *partial.shape[1:])
    return lax.all_to_all(pieces, axis, 0, 0, tiled=True).sum(0)


def shards(block_values, block_rows, block_cols, block_counts, right_side, ridge, n_comp, n_feat):
    values = block_values[0, 0]
    slot_rows = block_rows[0, 0]
    slot_cols = block_cols[0, 0]
    count_of_slots = block_counts[0, 0]
    responses = right_side.shape[1]
    block_edge = values.shape[1]
    feat_rows = CB_DEV * block_edge
    own_rows = feat_rows // n_comp
    comp_index = lax.axis_index("comp")

    def backward(low_slab):
        return block_apply(values, count_of_slots, slot_cols, slot_rows, low_slab, CB_DEV, True)

    def forward(direction, extra=None):
        low = direction.astype(jnp.bfloat16)
        if extra is None:
            summed = block_apply(values, count_of_slots, slot_rows, slot_cols, low, RB_DEV, False)
            return reduce_over(summed, "feat", n_feat)
        padded = jnp.zeros((8, extra.shape[1]), extra.dtype).at[: extra.shape[0]].set(extra)
        summed = block_apply(
            values, count_of_slots, slot_rows, slot_cols, low, RB_DEV, False, extra=padded
        )
        landed = reduce_over(summed, "feat", n_feat)
        return landed[:block_edge], landed[block_edge : block_edge + extra.shape[0]]

    core = comp_index % 2
    chip = comp_index // 2
    n_chips = n_comp // 2
    half_rows = feat_rows // 2
    siblings = [(i, i ^ 1) for i in range(n_comp)]
    same_core = [[i for i in range(n_comp) if i % 2 == p] for p in range(2)]

    def swap_with_sibling(x):
        return lax.ppermute(x, "comp", siblings)

    def reduce_gradient(partial):
        kept = lax.dynamic_slice_in_dim(partial, core * half_rows, half_rows, axis=0)
        sent = lax.dynamic_slice_in_dim(partial, (1 - core) * half_rows, half_rows, axis=0)
        chip_sum = kept + swap_with_sibling(sent)
        pieces = chip_sum.reshape(n_chips, own_rows, chip_sum.shape[1])
        landed = lax.all_to_all(pieces, "comp", 0, 0, tiled=True, axis_index_groups=same_core)
        return landed.sum(0)

    def gather_gradient(own):
        got = lax.all_gather(own, "comp", axis=0, tiled=False)
        by_chip = got[:, :own_rows].reshape(n_chips, 2, own_rows, own.shape[1])
        rows = by_chip.transpose(1, 0, 2, 3).reshape(feat_rows, own.shape[1])
        return rows, jnp.sum(got[:, own_rows:], axis=0)

    def own_part(full):
        return lax.dynamic_slice_in_dim(full, core * half_rows + chip * own_rows, own_rows, axis=0)

    def col_sq(x):
        return jnp.sum(x * x, axis=0)

    feat_index = lax.axis_index("feat")

    def gather_feat(own):
        spread = jnp.broadcast_to(own[None], (n_feat,) + own.shape)
        return lax.all_to_all(spread, "feat", 0, 0, tiled=True)

    def comp_total(stacked):
        spread = jnp.broadcast_to(stacked[None], (n_comp,) + stacked.shape)
        return lax.all_to_all(spread, "comp", 0, 0, tiled=True).sum(0)

    own_block = right_side.shape[0]
    residual_slab = gather_feat(right_side).reshape(RB_DEV * own_block, responses)

    def low_slab(slab):
        return slab.astype(jnp.bfloat16)

    gradient_own = reduce_gradient(backward(low_slab(residual_slab)))
    energy_own = col_sq(gradient_own)
    direction, _ = gather_gradient(gradient_own)
    energy = None
    solution = None
    for step_index in range(ITERS):
        last = step_index + 1 == ITERS
        if step_index > 0:
            gradient_own = reduce_gradient(backward(low_slab(residual_slab))) - ridge * own_part(
                solution
            )
            gradient, comp_energy = gather_gradient(
                jnp.concatenate([gradient_own, col_sq(gradient_own)[None]], axis=0)
            )
            gradient_image, next_energy = forward(gradient, comp_energy)
            next_energy = next_energy[0]
            conjugate = next_energy / energy
            direction = gradient + conjugate * direction
            image_rows = gradient_image + conjugate * image_rows
            energy = next_energy
        else:
            image_rows = forward(direction)
        if last:
            sums = [col_sq(image_rows), col_sq(own_part(direction))]
            if energy is None:
                sums.append(energy_own)
            spread = jnp.broadcast_to(jnp.stack(sums)[None], (n_feat, len(sums), responses))
            totals = comp_total(lax.all_to_all(spread, "feat", 0, 0, tiled=True).sum(0))
            if energy is None:
                energy = totals[2]
            image_energy, direction_energy = totals[0], totals[1]
        else:
            parts = [image_rows, col_sq(own_part(direction))[None]]
            if energy is None:
                parts.append(energy_own[None])
            gathered = gather_feat(jnp.concatenate(parts, axis=0))
            image_slab = gathered[:, :own_block].reshape(RB_DEV * own_block, responses)
            feat_sums = jnp.sum(gathered[:, own_block:], axis=0)
            totals = comp_total(jnp.concatenate([col_sq(image_slab)[None], feat_sums], axis=0))
            if energy is None:
                energy = totals[2]
            image_energy, direction_energy = totals[0], totals[1]
        step_size = energy / (image_energy + ridge * direction_energy)
        solution = step_size * direction if solution is None else solution + step_size * direction
        if last:
            own_residual = lax.dynamic_slice_in_dim(residual_slab, feat_index * own_block, own_block)
            residual = own_residual - step_size * image_rows
        else:
            residual_slab = residual_slab - step_size * image_slab
            image_rows = lax.dynamic_slice_in_dim(image_slab, feat_index * own_block, own_block)
    return (solution, residual)


def solution(mesh):
    placed = (
        P("comp", "feat", None, None, None),
        P("comp", "feat", None),
        P("comp", "feat", None),
        P("comp", "feat"),
        P(("comp", "feat"), None),
        P(),
    )
    n_comp = mesh.shape["comp"]
    n_feat = mesh.shape["feat"]

    def body(*args):
        return shards(*args, n_comp=n_comp, n_feat=n_feat)

    return jax.shard_map(
        body,
        mesh=mesh,
        in_specs=placed,
        out_specs=(P("feat", None), P(("comp", "feat"), None)),
        check_vma=False,
    )
```

```python
import functools

import jax
import jax.numpy as jnp
from jax import lax
from jax.experimental import pallas as pl
from jax.experimental.pallas import tpu as pltpu
from jax.sharding import PartitionSpec as P

RB_DEV = 16
CB_DEV = 14
ITERS = 2


def _block_kernel(transpose, pitch, keep_first, count_ref, out_idx_ref, in_idx_ref, core_ref, values_ref, x_ref, *rest):
    edge = values_ref.shape[1]
    out_ref = rest[-1]
    out_ref[...] = jnp.zeros_like(out_ref)
    if len(rest) == 2:
        extra_ref = rest[0]
        for b in range(out_ref.shape[0] // pitch):
            out_ref[pl.ds(b * pitch + edge, pitch - edge), :] = extra_ref[...]

    def body(s, carry):
        src = pl.multiple_of(in_idx_ref[s] * edge, edge)
        block_index = out_idx_ref[s]
        if keep_first:
            half = out_ref.shape[0] // pitch // 2
            other = (block_index // half != core_ref[0]).astype(jnp.int32)
            block_index = block_index % half + other * half
        dst = pl.multiple_of(block_index * pitch, 8)
        block = values_ref[s]
        x = x_ref[pl.ds(src, edge), :]
        if transpose:
            prod = lax.dot_general(
                block, x, (((0,), (0,)), ((), ())), preferred_element_type=jnp.float32
            )
        else:
            prod = jnp.dot(block, x, preferred_element_type=jnp.float32)
        live = s < count_ref[0]
        out_ref[pl.ds(dst, edge), :] += jnp.where(live, prod, 0.0)
        return carry

    lax.fori_loop(0, values_ref.shape[0], body, 0, unroll=True)


def block_apply(values, count, out_idx, in_idx, x, out_blocks, transpose, extra=None, core=None):
    edge = values.shape[1]
    pitch = edge if extra is None else edge + extra.shape[0]
    smem = pl.BlockSpec(memory_space=pltpu.SMEM)
    vmem = pl.BlockSpec(memory_space=pltpu.VMEM)
    keep_first = core is not None
    core = jnp.zeros((1,), jnp.int32) if core is None else core.astype(jnp.int32).reshape(1)
    operands = [count.reshape(1), out_idx, in_idx, core, values, x]
    if extra is not None:
        operands.append(extra)
    return pl.pallas_call(
        functools.partial(_block_kernel, transpose, pitch, keep_first),
        out_shape=jax.ShapeDtypeStruct((out_blocks * pitch, x.shape[1]), jnp.float32),
        in_specs=[smem, smem, smem, smem] + [vmem] * (len(operands) - 4),
        out_specs=vmem,
    )(*operands)


def reduce_over(partial, axis, parts):
    rows = partial.shape[0] // parts
    pieces = partial.reshape(parts, rows, *partial.shape[1:])
    return lax.all_to_all(pieces, axis, 0, 0, tiled=True).sum(0)


def shards(block_values, block_rows, block_cols, block_counts, right_side, ridge, n_comp, n_feat):
    values = block_values[0, 0]
    slot_rows = block_rows[0, 0]
    slot_cols = block_cols[0, 0]
    count_of_slots = block_counts[0, 0]
    responses = right_side.shape[1]
    block_edge = values.shape[1]
    feat_rows = CB_DEV * block_edge
    own_rows = feat_rows // n_comp
    comp_index = lax.axis_index("comp")
    core = comp_index % 2

    def backward(low_slab):
        return block_apply(
            values, count_of_slots, slot_cols, slot_rows, low_slab, CB_DEV, True, core=core
        )

    def forward(direction, extra=None):
        low = direction.astype(jnp.bfloat16)
        if extra is None:
            summed = block_apply(values, count_of_slots, slot_rows, slot_cols, low, RB_DEV, False)
            return reduce_over(summed, "feat", n_feat)
        padded = jnp.zeros((8, extra.shape[1]), extra.dtype).at[: extra.shape[0]].set(extra)
        summed = block_apply(
            values, count_of_slots, slot_rows, slot_cols, low, RB_DEV, False, extra=padded
        )
        landed = reduce_over(summed, "feat", n_feat)
        return landed[:block_edge], landed[block_edge : block_edge + extra.shape[0]]

    chip = comp_index // 2
    n_chips = n_comp // 2
    half_rows = feat_rows // 2
    siblings = [(i, i ^ 1) for i in range(n_comp)]
    same_core = [[i for i in range(n_comp) if i % 2 == p] for p in range(2)]

    def swap_with_sibling(x):
        return lax.ppermute(x, "comp", siblings)

    def reduce_gradient(partial):
        kept, sent = partial[:half_rows], partial[half_rows:]
        chip_sum = kept + swap_with_sibling(sent)
        pieces = chip_sum.reshape(n_chips, own_rows, chip_sum.shape[1])
        landed = lax.all_to_all(pieces, "comp", 0, 0, tiled=True, axis_index_groups=same_core)
        return landed.sum(0)

    def gather_gradient(own):
        got = lax.all_gather(own, "comp", axis=0, tiled=False)
        by_chip = got[:, :own_rows].reshape(n_chips, 2, own_rows, own.shape[1])
        rows = by_chip.transpose(1, 0, 2, 3).reshape(feat_rows, own.shape[1])
        return rows, jnp.sum(got[:, own_rows:], axis=0)

    def own_part(full):
        return lax.dynamic_slice_in_dim(full, core * half_rows + chip * own_rows, own_rows, axis=0)

    def col_sq(x):
        return jnp.sum(x * x, axis=0)

    feat_index = lax.axis_index("feat")

    def gather_feat(own):
        spread = jnp.broadcast_to(own[None], (n_feat,) + own.shape)
        return lax.all_to_all(spread, "feat", 0, 0, tiled=True)

    def comp_total(stacked):
        spread = jnp.broadcast_to(stacked[None], (n_comp,) + stacked.shape)
        return lax.all_to_all(spread, "comp", 0, 0, tiled=True).sum(0)

    own_block = right_side.shape[0]
    residual_slab = gather_feat(right_side).reshape(RB_DEV * own_block, responses)

    def low_slab(slab):
        return slab.astype(jnp.bfloat16)

    gradient_own = reduce_gradient(backward(low_slab(residual_slab)))
    energy_own = col_sq(gradient_own)
    direction, _ = gather_gradient(gradient_own)
    energy = None
    solution = None
    for step_index in range(ITERS):
        last = step_index + 1 == ITERS
        if step_index > 0:
            gradient_own = reduce_gradient(backward(low_slab(residual_slab))) - ridge * own_part(
                solution
            )
            gradient, comp_energy = gather_gradient(
                jnp.concatenate([gradient_own, col_sq(gradient_own)[None]], axis=0)
            )
            gradient_image, next_energy = forward(gradient, comp_energy)
            next_energy = next_energy[0]
            conjugate = next_energy / energy
            direction = gradient + conjugate * direction
            image_rows = gradient_image + conjugate * image_rows
            energy = next_energy
        else:
            image_rows = forward(direction)
        if last:
            sums = [col_sq(image_rows), col_sq(own_part(direction))]
            if energy is None:
                sums.append(energy_own)
            spread = jnp.broadcast_to(jnp.stack(sums)[None], (n_feat, len(sums), responses))
            totals = comp_total(lax.all_to_all(spread, "feat", 0, 0, tiled=True).sum(0))
            if energy is None:
                energy = totals[2]
            image_energy, direction_energy = totals[0], totals[1]
        else:
            parts = [image_rows, col_sq(own_part(direction))[None]]
            if energy is None:
                parts.append(energy_own[None])
            gathered = gather_feat(jnp.concatenate(parts, axis=0))
            image_slab = gathered[:, :own_block].reshape(RB_DEV * own_block, responses)
            feat_sums = jnp.sum(gathered[:, own_block:], axis=0)
            totals = comp_total(jnp.concatenate([col_sq(image_slab)[None], feat_sums], axis=0))
            if energy is None:
                energy = totals[2]
            image_energy, direction_energy = totals[0], totals[1]
        step_size = energy / (image_energy + ridge * direction_energy)
        solution = step_size * direction if solution is None else solution + step_size * direction
        if last:
            own_residual = lax.dynamic_slice_in_dim(residual_slab, feat_index * own_block, own_block)
            residual = own_residual - step_size * image_rows
        else:
            residual_slab = residual_slab - step_size * image_slab
            image_rows = lax.dynamic_slice_in_dim(image_slab, feat_index * own_block, own_block)
    return (solution, residual)


def solution(mesh):
    placed = (
        P("comp", "feat", None, None, None),
        P("comp", "feat", None),
        P("comp", "feat", None),
        P("comp", "feat"),
        P(("comp", "feat"), None),
        P(),
    )
    n_comp = mesh.shape["comp"]
    n_feat = mesh.shape["feat"]

    def body(*args):
        return shards(*args, n_comp=n_comp, n_feat=n_feat)

    return jax.shard_map(
        body,
        mesh=mesh,
        in_specs=placed,
        out_specs=(P("feat", None), P(("comp", "feat"), None)),
        check_vma=False,
    )
```

```python
import functools

import jax
import jax.numpy as jnp
from jax import lax
from jax.experimental import pallas as pl
from jax.experimental.pallas import tpu as pltpu
from jax.sharding import PartitionSpec as P

RB_DEV = 16
CB_DEV = 14
ITERS = 2


def _block_kernel(transpose, pitch, count_ref, out_idx_ref, in_idx_ref, values_ref, x_ref, *rest):
    edge = values_ref.shape[1]
    out_ref = rest[-1]
    out_ref[...] = jnp.zeros_like(out_ref)
    if len(rest) == 2:
        extra_ref = rest[0]
        for b in range(out_ref.shape[0] // pitch):
            out_ref[pl.ds(b * pitch + edge, pitch - edge), :] = extra_ref[...]

    def body(s, carry):
        src = pl.multiple_of(in_idx_ref[s] * edge, edge)
        dst = pl.multiple_of(out_idx_ref[s] * pitch, 8)
        block = values_ref[s]
        x = x_ref[pl.ds(src, edge), :]
        if transpose:
            prod = lax.dot_general(
                block, x, (((0,), (0,)), ((), ())), preferred_element_type=jnp.float32
            )
        else:
            prod = jnp.dot(block, x, preferred_element_type=jnp.float32)
        live = s < count_ref[0]
        out_ref[pl.ds(dst, edge), :] += jnp.where(live, prod, 0.0)
        return carry

    lax.fori_loop(0, values_ref.shape[0], body, 0, unroll=True)


def block_apply(values, count, out_idx, in_idx, x, out_blocks, transpose, extra=None):
    edge = values.shape[1]
    pitch = edge if extra is None else edge + extra.shape[0]
    smem = pl.BlockSpec(memory_space=pltpu.SMEM)
    vmem = pl.BlockSpec(memory_space=pltpu.VMEM)
    operands = [count.reshape(1), out_idx, in_idx, values, x]
    if extra is not None:
        operands.append(extra)
    return pl.pallas_call(
        functools.partial(_block_kernel, transpose, pitch),
        out_shape=jax.ShapeDtypeStruct((out_blocks * pitch, x.shape[1]), jnp.float32),
        in_specs=[smem, smem, smem] + [vmem] * (len(operands) - 3),
        out_specs=vmem,
    )(*operands)


def reduce_over(partial, axis, parts):
    rows = partial.shape[0] // parts
    pieces = partial.reshape(parts, rows, *partial.shape[1:])
    return lax.all_to_all(pieces, axis, 0, 0, tiled=True).sum(0)


def shards(block_values, block_rows, block_cols, block_counts, right_side, ridge, n_comp, n_feat):
    values = block_values[0, 0]
    slot_rows = block_rows[0, 0]
    slot_cols = block_cols[0, 0]
    count_of_slots = block_counts[0, 0]
    responses = right_side.shape[1]
    block_edge = values.shape[1]
    feat_rows = CB_DEV * block_edge
    own_rows = feat_rows // n_comp
    comp_index = lax.axis_index("comp")

    def backward(low_slab):
        return block_apply(values, count_of_slots, slot_cols, slot_rows, low_slab, CB_DEV, True)

    def forward(direction, extra=None):
        low = direction.astype(jnp.bfloat16)
        if extra is None:
            summed = block_apply(values, count_of_slots, slot_rows, slot_cols, low, RB_DEV, False)
            return reduce_over(summed, "feat", n_feat)
        padded = jnp.zeros((8, extra.shape[1]), extra.dtype).at[: extra.shape[0]].set(extra)
        summed = block_apply(
            values, count_of_slots, slot_rows, slot_cols, low, RB_DEV, False, extra=padded
        )
        landed = reduce_over(summed, "feat", n_feat)
        return landed[:block_edge], landed[block_edge : block_edge + extra.shape[0]]

    core = comp_index % 2
    chip = comp_index // 2
    n_chips = n_comp // 2
    half_rows = feat_rows // 2
    siblings = [(i, i ^ 1) for i in range(n_comp)]
    same_core = [[i for i in range(n_comp) if i % 2 == p] for p in range(2)]

    def swap_with_sibling(x):
        return lax.ppermute(x, "comp", siblings)

    def reduce_gradient(partial):
        kept = lax.dynamic_slice_in_dim(partial, core * half_rows, half_rows, axis=0)
        sent = lax.dynamic_slice_in_dim(partial, (1 - core) * half_rows, half_rows, axis=0)
        chip_sum = kept + swap_with_sibling(sent)
        pieces = chip_sum.reshape(n_chips, own_rows, chip_sum.shape[1])
        landed = lax.all_to_all(pieces, "comp", 0, 0, tiled=True, axis_index_groups=same_core)
        return landed.sum(0)

    def gather_gradient(own):
        got = lax.all_gather(own, "comp", axis=0, tiled=False)
        by_chip = got[:, :own_rows].reshape(n_chips, 2, own_rows, own.shape[1])
        rows = by_chip.transpose(1, 0, 2, 3).reshape(feat_rows, own.shape[1])
        return rows, jnp.sum(got[:, own_rows:], axis=0)

    def own_part(full):
        return lax.dynamic_slice_in_dim(full, core * half_rows + chip * own_rows, own_rows, axis=0)

    def col_sq(x):
        return jnp.sum(x * x, axis=0)

    feat_index = lax.axis_index("feat")

    def gather_feat(own):
        spread = jnp.broadcast_to(own[None], (n_feat,) + own.shape)
        return lax.all_to_all(spread, "feat", 0, 0, tiled=True)

    def comp_total(stacked):
        spread = jnp.broadcast_to(stacked[None], (n_comp,) + stacked.shape)
        return lax.all_to_all(spread, "comp", 0, 0, tiled=True).sum(0)

    own_block = right_side.shape[0]
    residual_slab = gather_feat(right_side).reshape(RB_DEV * own_block, responses)

    def low_slab(slab):
        return slab.astype(jnp.bfloat16)

    gradient_own = reduce_gradient(backward(low_slab(residual_slab)))
    energy_own = col_sq(gradient_own)
    direction, _ = gather_gradient(gradient_own)
    energy = None
    solution = None
    own_residual = right_side
    for step_index in range(ITERS):
        last = step_index + 1 == ITERS
        if step_index > 0:
            gradient_own = reduce_gradient(backward(low_slab(residual_slab))) - ridge * own_part(
                solution
            )
            gradient, comp_energy = gather_gradient(
                jnp.concatenate([gradient_own, col_sq(gradient_own)[None]], axis=0)
            )
            gradient_image, next_energy = forward(gradient, comp_energy)
            next_energy = next_energy[0]
            conjugate = next_energy / energy
            direction = gradient + conjugate * direction
            image_rows = gradient_image + conjugate * image_rows
            energy = next_energy
        else:
            image_rows = forward(direction)
        if last:
            sums = [col_sq(image_rows), col_sq(own_part(direction))]
            if energy is None:
                sums.append(energy_own)
            spread = jnp.broadcast_to(jnp.stack(sums)[None], (n_feat, len(sums), responses))
            totals = comp_total(lax.all_to_all(spread, "feat", 0, 0, tiled=True).sum(0))
            if energy is None:
                energy = totals[2]
            image_energy, direction_energy = totals[0], totals[1]
        else:
            parts = [image_rows, col_sq(own_part(direction))[None]]
            if energy is None:
                parts.append(energy_own[None])
            gathered = gather_feat(jnp.concatenate(parts, axis=0))
            image_slab = gathered[:, :own_block].reshape(RB_DEV * own_block, responses)
            feat_sums = jnp.sum(gathered[:, own_block:], axis=0)
            totals = comp_total(jnp.concatenate([col_sq(image_slab)[None], feat_sums], axis=0))
            if energy is None:
                energy = totals[2]
            image_energy, direction_energy = totals[0], totals[1]
        step_size = energy / (image_energy + ridge * direction_energy)
        solution = step_size * direction if solution is None else solution + step_size * direction
        if last:
            residual = own_residual - step_size * image_rows
        else:
            own_residual = own_residual - step_size * image_rows
            residual_slab = residual_slab - step_size * image_slab
    return (solution, residual)


def solution(mesh):
    placed = (
        P("comp", "feat", None, None, None),
        P("comp", "feat", None),
        P("comp", "feat", None),
        P("comp", "feat"),
        P(("comp", "feat"), None),
        P(),
    )
    n_comp = mesh.shape["comp"]
    n_feat = mesh.shape["feat"]

    def body(*args):
        return shards(*args, n_comp=n_comp, n_feat=n_feat)

    return jax.shard_map(
        body,
        mesh=mesh,
        in_specs=placed,
        out_specs=(P("feat", None), P(("comp", "feat"), None)),
        check_vma=False,
    )
```

```python
import functools

import jax
import jax.numpy as jnp
from jax import lax
from jax.experimental import pallas as pl
from jax.experimental.pallas import tpu as pltpu
from jax.sharding import PartitionSpec as P

RB_DEV = 16
CB_DEV = 14
ITERS = 2


def _block_kernel(transpose, pitch, count_ref, out_idx_ref, in_idx_ref, values_ref, x_ref, *rest):
    edge = values_ref.shape[1]
    out_ref = rest[-1]
    out_ref[...] = jnp.zeros_like(out_ref)
    if len(rest) == 2:
        extra_ref = rest[0]
        for b in range(out_ref.shape[0] // pitch):
            out_ref[pl.ds(b * pitch + edge, pitch - edge), :] = extra_ref[...]

    def body(s, carry):
        src = pl.multiple_of(in_idx_ref[s] * edge, edge)
        dst = pl.multiple_of(out_idx_ref[s] * pitch, 8)
        block = values_ref[s]
        x = x_ref[pl.ds(src, edge), :]
        if transpose:
            prod = lax.dot_general(
                block, x, (((0,), (0,)), ((), ())), preferred_element_type=jnp.float32
            )
        else:
            prod = jnp.dot(block, x, preferred_element_type=jnp.float32)
        live = s < count_ref[0]
        out_ref[pl.ds(dst, edge), :] += jnp.where(live, prod, 0.0)
        return carry

    lax.fori_loop(0, values_ref.shape[0], body, 0, unroll=True)


def block_apply(values, count, out_idx, in_idx, x, out_blocks, transpose, extra=None):
    edge = values.shape[1]
    pitch = edge if extra is None else edge + extra.shape[0]
    smem = pl.BlockSpec(memory_space=pltpu.SMEM)
    vmem = pl.BlockSpec(memory_space=pltpu.VMEM)
    operands = [count.reshape(1), out_idx, in_idx, values, x]
    if extra is not None:
        operands.append(extra)
    return pl.pallas_call(
        functools.partial(_block_kernel, transpose, pitch),
        out_shape=jax.ShapeDtypeStruct((out_blocks * pitch, x.shape[1]), jnp.float32),
        in_specs=[smem, smem, smem] + [vmem] * (len(operands) - 3),
        out_specs=vmem,
    )(*operands)


def reduce_over(partial, axis, parts):
    rows = partial.shape[0] // parts
    pieces = partial.reshape(parts, rows, *partial.shape[1:])
    return lax.all_to_all(pieces, axis, 0, 0, tiled=True).sum(0)


def shards(block_values, block_rows, block_cols, block_counts, right_side, ridge, n_comp, n_feat):
    values = block_values[0, 0]
    slot_rows = block_rows[0, 0]
    slot_cols = block_cols[0, 0]
    count_of_slots = block_counts[0, 0]
    responses = right_side.shape[1]
    block_edge = values.shape[1]
    feat_rows = CB_DEV * block_edge
    own_rows = feat_rows // n_comp
    comp_index = lax.axis_index("comp")

    def backward(low_slab):
        return block_apply(values, count_of_slots, slot_cols, slot_rows, low_slab, CB_DEV, True)

    def forward(direction, extra=None):
        low = direction.astype(jnp.bfloat16)
        if extra is None:
            summed = block_apply(values, count_of_slots, slot_rows, slot_cols, low, RB_DEV, False)
            return reduce_over(summed, "feat", n_feat)
        padded = jnp.zeros((8, extra.shape[1]), extra.dtype).at[: extra.shape[0]].set(extra)
        summed = block_apply(
            values, count_of_slots, slot_rows, slot_cols, low, RB_DEV, False, extra=padded
        )
        landed = reduce_over(summed, "feat", n_feat)
        return landed[:block_edge], landed[block_edge : block_edge + extra.shape[0]]

    core = comp_index % 2
    chip = comp_index // 2
    n_chips = n_comp // 2
    half_rows = feat_rows // 2
    siblings = [(i, i ^ 1) for i in range(n_comp)]
    same_core = [[i for i in range(n_comp) if i % 2 == p] for p in range(2)]

    def swap_with_sibling(x):
        return lax.ppermute(x, "comp", siblings)

    def reduce_gradient(partial):
        kept = lax.dynamic_slice_in_dim(partial, core * half_rows, half_rows, axis=0)
        sent = lax.dynamic_slice_in_dim(partial, (1 - core) * half_rows, half_rows, axis=0)
        chip_sum = kept + swap_with_sibling(sent)
        pieces = chip_sum.reshape(n_chips, own_rows, chip_sum.shape[1])
        landed = lax.all_to_all(pieces, "comp", 0, 0, tiled=True, axis_index_groups=same_core)
        return landed.sum(0)

    def gather_gradient(own):
        got = lax.all_gather(own, "comp", axis=0, tiled=False)
        by_chip = got[:, :own_rows].reshape(n_chips, 2, own_rows, own.shape[1])
        rows = by_chip.transpose(1, 0, 2, 3).reshape(feat_rows, own.shape[1])
        return rows, jnp.sum(got[:, own_rows:], axis=0)

    def own_part(full):
        return lax.dynamic_slice_in_dim(full, core * half_rows + chip * own_rows, own_rows, axis=0)

    def col_sq(x):
        return jnp.sum(x * x, axis=0)

    feat_index = lax.axis_index("feat")

    def gather_feat(own):
        spread = jnp.broadcast_to(own[None], (n_feat,) + own.shape)
        return lax.all_to_all(spread, "feat", 0, 0, tiled=True)

    def comp_total(stacked):
        spread = jnp.broadcast_to(stacked[None], (n_comp,) + stacked.shape)
        return lax.all_to_all(spread, "comp", 0, 0, tiled=True).sum(0)

    own_block = right_side.shape[0]
    residual_slab = gather_feat(right_side).reshape(RB_DEV * own_block, responses)

    def low_slab(slab):
        return slab.astype(jnp.bfloat16)

    gradient_own = reduce_gradient(backward(low_slab(residual_slab)))
    energy_own = col_sq(gradient_own)
    direction, _ = gather_gradient(gradient_own)
    energy = None
    solution = None
    own_residual = right_side
    for step_index in range(ITERS):
        last = step_index + 1 == ITERS
        if step_index > 0:
            gradient_own = reduce_gradient(backward(low_slab(residual_slab))) - ridge * own_part(
                solution
            )
            gradient, comp_energy = gather_gradient(
                jnp.concatenate([gradient_own, col_sq(gradient_own)[None]], axis=0)
            )
            gradient_image, next_energy = forward(gradient, comp_energy)
            next_energy = next_energy[0]
            conjugate = next_energy / energy
            direction = gradient + conjugate * direction
            image_rows = gradient_image + conjugate * image_rows
            energy = next_energy
        else:
            image_rows = forward(direction)
        if last:
            sums = [col_sq(image_rows), col_sq(own_part(direction))]
            if energy is None:
                sums.append(energy_own)
            spread = jnp.broadcast_to(jnp.stack(sums)[None], (n_feat, len(sums), responses))
            totals = comp_total(lax.all_to_all(spread, "feat", 0, 0, tiled=True).sum(0))
            if energy is None:
                energy = totals[2]
            image_energy, direction_energy = totals[0], totals[1]
        else:
            own_energy = energy_own if energy is None else col_sq(own_part(direction))
            gathered = gather_feat(jnp.concatenate([image_rows, own_energy[None]], axis=0))
            image_slab = gathered[:, :own_block].reshape(RB_DEV * own_block, responses)
            feat_sums = jnp.sum(gathered[:, own_block:], axis=0)
            totals = comp_total(jnp.concatenate([col_sq(image_slab)[None], feat_sums], axis=0))
            if energy is None:
                energy = totals[1]
            image_energy, direction_energy = totals[0], totals[1]
        step_size = energy / (image_energy + ridge * direction_energy)
        solution = step_size * direction if solution is None else solution + step_size * direction
        if last:
            residual = own_residual - step_size * image_rows
        else:
            own_residual = own_residual - step_size * image_rows
            residual_slab = residual_slab - step_size * image_slab
    return (solution, residual)


def solution(mesh):
    placed = (
        P("comp", "feat", None, None, None),
        P("comp", "feat", None),
        P("comp", "feat", None),
        P("comp", "feat"),
        P(("comp", "feat"), None),
        P(),
    )
    n_comp = mesh.shape["comp"]
    n_feat = mesh.shape["feat"]

    def body(*args):
        return shards(*args, n_comp=n_comp, n_feat=n_feat)

    return jax.shard_map(
        body,
        mesh=mesh,
        in_specs=placed,
        out_specs=(P("feat", None), P(("comp", "feat"), None)),
        check_vma=False,
    )
```

```python
import functools

import jax
import jax.numpy as jnp
from jax import lax
from jax.experimental import pallas as pl
from jax.experimental.pallas import tpu as pltpu
from jax.sharding import PartitionSpec as P

RB_DEV = 16
CB_DEV = 14
ITERS = 2


def _block_kernel(transpose, pitch, count_ref, out_idx_ref, in_idx_ref, values_ref, x_ref, *rest):
    edge = values_ref.shape[1]
    out_ref = rest[-1]
    out_ref[...] = jnp.zeros_like(out_ref)
    if len(rest) == 2:
        extra_ref = rest[0]
        for b in range(out_ref.shape[0] // pitch):
            out_ref[pl.ds(b * pitch + edge, pitch - edge), :] = extra_ref[...]

    def body(s, carry):
        src = pl.multiple_of(in_idx_ref[s] * edge, edge)
        dst = pl.multiple_of(out_idx_ref[s] * pitch, 8)
        block = values_ref[s]
        x = x_ref[pl.ds(src, edge), :]
        if transpose:
            prod = lax.dot_general(
                block, x, (((0,), (0,)), ((), ())), preferred_element_type=jnp.float32
            )
        else:
            prod = jnp.dot(block, x, preferred_element_type=jnp.float32)
        live = s < count_ref[0]
        out_ref[pl.ds(dst, edge), :] += jnp.where(live, prod, 0.0)
        return carry

    lax.fori_loop(0, values_ref.shape[0], body, 0, unroll=True)


def block_apply(values, count, out_idx, in_idx, x, out_blocks, transpose, extra=None):
    edge = values.shape[1]
    pitch = edge if extra is None else edge + extra.shape[0]
    smem = pl.BlockSpec(memory_space=pltpu.SMEM)
    vmem = pl.BlockSpec(memory_space=pltpu.VMEM)
    operands = [count.reshape(1), out_idx, in_idx, values, x]
    if extra is not None:
        operands.append(extra)
    return pl.pallas_call(
        functools.partial(_block_kernel, transpose, pitch),
        out_shape=jax.ShapeDtypeStruct((out_blocks * pitch, x.shape[1]), jnp.float32),
        in_specs=[smem, smem, smem] + [vmem] * (len(operands) - 3),
        out_specs=vmem,
    )(*operands)


def reduce_over(partial, axis, parts):
    rows = partial.shape[0] // parts
    pieces = partial.reshape(parts, rows, *partial.shape[1:])
    return lax.all_to_all(pieces, axis, 0, 0, tiled=True).sum(0)


def shards(block_values, block_rows, block_cols, block_counts, right_side, ridge, n_comp, n_feat):
    values = block_values[0, 0]
    slot_rows = block_rows[0, 0]
    slot_cols = block_cols[0, 0]
    count_of_slots = block_counts[0, 0]
    responses = right_side.shape[1]
    block_edge = values.shape[1]
    feat_rows = CB_DEV * block_edge
    own_rows = feat_rows // n_comp
    comp_index = lax.axis_index("comp")

    def backward(low_slab):
        return block_apply(values, count_of_slots, slot_cols, slot_rows, low_slab, CB_DEV, True)

    def forward(direction, extra=None):
        low = direction.astype(jnp.bfloat16)
        if extra is None:
            summed = block_apply(values, count_of_slots, slot_rows, slot_cols, low, RB_DEV, False)
            return reduce_over(summed, "feat", n_feat)
        padded = jnp.zeros((8, extra.shape[1]), extra.dtype).at[: extra.shape[0]].set(extra)
        summed = block_apply(
            values, count_of_slots, slot_rows, slot_cols, low, RB_DEV, False, extra=padded
        )
        landed = reduce_over(summed, "feat", n_feat)
        return landed[:block_edge], landed[block_edge : block_edge + extra.shape[0]]

    core = comp_index % 2
    chip = comp_index // 2
    n_chips = n_comp // 2
    half_rows = feat_rows // 2
    siblings = [(i, i ^ 1) for i in range(n_comp)]
    same_core = [[i for i in range(n_comp) if i % 2 == p] for p in range(2)]

    def swap_with_sibling(x):
        return lax.ppermute(x, "comp", siblings)

    def reduce_gradient(partial):
        kept = lax.dynamic_slice_in_dim(partial, core * half_rows, half_rows, axis=0)
        sent = lax.dynamic_slice_in_dim(partial, (1 - core) * half_rows, half_rows, axis=0)
        chip_sum = kept + swap_with_sibling(sent)
        pieces = chip_sum.reshape(n_chips, own_rows, chip_sum.shape[1])
        landed = lax.all_to_all(pieces, "comp", 0, 0, tiled=True, axis_index_groups=same_core)
        return landed.sum(0)

    def gather_gradient(own):
        got = lax.all_gather(own, "comp", axis=0, tiled=False)
        by_chip = got[:, :own_rows].reshape(n_chips, 2, own_rows, own.shape[1])
        rows = by_chip.transpose(1, 0, 2, 3).reshape(feat_rows, own.shape[1])
        return rows, jnp.sum(got[:, own_rows:], axis=0)

    def own_part(full):
        return lax.dynamic_slice_in_dim(full, core * half_rows + chip * own_rows, own_rows, axis=0)

    def col_sq(x):
        return jnp.sum(x * x, axis=0)

    feat_index = lax.axis_index("feat")

    def gather_feat(own):
        spread = jnp.broadcast_to(own[None], (n_feat,) + own.shape)
        return lax.all_to_all(spread, "feat", 0, 0, tiled=True)

    def comp_total(stacked):
        spread = jnp.broadcast_to(stacked[None], (n_comp,) + stacked.shape)
        return lax.all_to_all(spread, "comp", 0, 0, tiled=True).sum(0)

    own_block = right_side.shape[0]
    residual_slab = gather_feat(right_side).reshape(RB_DEV * own_block, responses)

    def low_slab(slab):
        return slab.astype(jnp.bfloat16)

    gradient_own = reduce_gradient(backward(low_slab(residual_slab)))
    energy_own = col_sq(gradient_own)
    direction, _ = gather_gradient(gradient_own)
    energy = None
    solution = None
    own_residual = right_side
    for step_index in range(ITERS):
        last = step_index + 1 == ITERS
        if step_index > 0:
            gradient_own = reduce_gradient(backward(low_slab(residual_slab))) - ridge * own_part(
                solution
            )
            energy_rows = jnp.zeros((8, responses), jnp.float32).at[0].set(col_sq(gradient_own))
            gradient, comp_energy = gather_gradient(
                jnp.concatenate([gradient_own, energy_rows], axis=0)
            )
            comp_energy = comp_energy[:1]
            gradient_image, next_energy = forward(gradient, comp_energy)
            next_energy = next_energy[0]
            conjugate = next_energy / energy
            direction = gradient + conjugate * direction
            image_rows = gradient_image + conjugate * image_rows
            energy = next_energy
        else:
            image_rows = forward(direction)
        if last:
            sums = [col_sq(image_rows), col_sq(own_part(direction))]
            if energy is None:
                sums.append(energy_own)
            spread = jnp.broadcast_to(jnp.stack(sums)[None], (n_feat, len(sums), responses))
            totals = comp_total(lax.all_to_all(spread, "feat", 0, 0, tiled=True).sum(0))
            if energy is None:
                energy = totals[2]
            image_energy, direction_energy = totals[0], totals[1]
        else:
            own_energy = energy_own if energy is None else col_sq(own_part(direction))
            gathered = gather_feat(jnp.concatenate([image_rows, own_energy[None]], axis=0))
            image_slab = gathered[:, :own_block].reshape(RB_DEV * own_block, responses)
            feat_sums = jnp.sum(gathered[:, own_block:], axis=0)
            totals = comp_total(jnp.concatenate([col_sq(image_slab)[None], feat_sums], axis=0))
            if energy is None:
                energy = totals[1]
            image_energy, direction_energy = totals[0], totals[1]
        step_size = energy / (image_energy + ridge * direction_energy)
        solution = step_size * direction if solution is None else solution + step_size * direction
        if last:
            residual = own_residual - step_size * image_rows
        else:
            own_residual = own_residual - step_size * image_rows
            residual_slab = residual_slab - step_size * image_slab
    return (solution, residual)


def solution(mesh):
    placed = (
        P("comp", "feat", None, None, None),
        P("comp", "feat", None),
        P("comp", "feat", None),
        P("comp", "feat"),
        P(("comp", "feat"), None),
        P(),
    )
    n_comp = mesh.shape["comp"]
    n_feat = mesh.shape["feat"]

    def body(*args):
        return shards(*args, n_comp=n_comp, n_feat=n_feat)

    return jax.shard_map(
        body,
        mesh=mesh,
        in_specs=placed,
        out_specs=(P("feat", None), P(("comp", "feat"), None)),
        check_vma=False,
    )
```
